32 devices in a mesh: row: 8 (over y, x, core), col: 4 (over z).
Axes of the slice: x: 2, y: 2, z: 4, core: 2. Of those that a mesh axis runs over, the one named last changes fastest.
Arguments:
- tokens: bfloat16 [192, 8192], P('col', 'row'), may hold values from -6 to 6
- grad_out: bfloat16 [192, 8192], P('col', 'row'), may hold values from -6 to 6
- gate_weight: bfloat16 [8192, 14336], P('row', 'col'), may hold values from -0.0625 to 0.0625
- up_weight: bfloat16 [8192, 14336], P('row', 'col'), may hold values from -0.0625 to 0.0625
- down_weight: bfloat16 [14336, 8192], P('col', 'row'), may hold values from -0.046875 to 0.046875
Outputs:
- grad_tokens: bfloat16 [192, 8192], P('col', 'row')
- grad_gate_weight: bfloat16 [8192, 14336], P('row', 'col')
- grad_up_weight: bfloat16 [8192, 14336], P('row', 'col')
- grad_down_weight: bfloat16 [14336, 8192], P('col', 'row')
The draws below stay inside these ranges and needn't reach their ends.
All inputs are finite; a program needn't handle non-finite values.
Results may differ from the reference program's by a relative error of at most 0.024.
Values may be sent and summed in bfloat16 or wider, within the bound.
No kernel may reach another device: no remote copies, remote signals or barrier semaphores. Data moves between devices by JAX's collectives and lax.ppermute only.
A program may use at most 128 MiB of HBM per device.

```python
import jax
import jax.numpy as jnp
from jax import lax

D = 8192
FF = 14336
TOKENS = 192
N_ROW = 8
N_COL = 4


def shard_levels(own_key, shape, cuts, low, high):
    loudness, own = 1.0, jax.random.fold_in(own_key, 6)
    for axis_at, shards_of in cuts:
        draws = jnp.exp(jax.random.uniform(jax.random.fold_in(own, axis_at), (shards_of,), jnp.float32, low / len(cuts), high / len(cuts)))
        loudness = loudness * jnp.repeat(draws, shape[axis_at] // shards_of).reshape([-1 if axis == axis_at else 1 for axis in range(len(shape))])
    return loudness


def bell_draw(key, dims, width, most, split=(), kind=jnp.bfloat16):
    entries = jax.random.normal(key, dims, jnp.float32) * width
    if len(split) > 0:
        entries = shard_levels(key, dims, split, -0.22, 0.18) * entries
    return jnp.clip(entries, min=-most, max=most).astype(kind)


def setup_inputs(seed: int = 0) -> dict:
    arg_keys = jax.random.split(jax.random.key(seed), 6)
    tokens = bell_draw(arg_keys[0], (TOKENS, D), 1.0, 6.0, ((0, 4), (1, 8)))
    grad_out = bell_draw(arg_keys[1], (TOKENS, D), 1.0, 6.0, ((0, 4), (1, 8)))
    gate_weight = bell_draw(arg_keys[2], (D, FF), D ** -0.5, 0.0625, ((0, 8), (1, 4)))
    up_weight = bell_draw(arg_keys[3], (D, FF), D ** -0.5, 0.0625, ((0, 8), (1, 4)))
    down_weight = bell_draw(arg_keys[4], (FF, D), FF ** -0.5, 0.046875, ((0, 4), (1, 8)))
    return dict(tokens=tokens, grad_out=grad_out, gate_weight=gate_weight, up_weight=up_weight, down_weight=down_weight)


def feature_block_sums(tokens, grad_out, gate_weight, up_weight, down_weight):
    block_span = D // N_ROW

    def scan_step(running, block_index):
        offset = (block_index * block_span).astype(jnp.int32)
        tok_rows = lax.dynamic_slice_in_dim(tokens, offset, block_span, 1)
        grad_rows = lax.dynamic_slice_in_dim(grad_out, offset, block_span, 1)
        gate_block = lax.dynamic_slice_in_dim(gate_weight, offset, block_span, 0)
        up_block = lax.dynamic_slice_in_dim(up_weight, offset, block_span, 0)
        down_block = lax.dynamic_slice_in_dim(down_weight, offset, block_span, 1)
        products = (jnp.dot(tok_rows, gate_block, preferred_element_type=jnp.float32),
                    jnp.dot(tok_rows, up_block, preferred_element_type=jnp.float32),
                    jnp.dot(grad_rows, down_block.T, preferred_element_type=jnp.float32))
        rounded = lax.optimization_barrier(tuple(p.astype(jnp.bfloat16) for p in products))
        return tuple(r + q.astype(jnp.float32) for r, q in zip(running, rounded)), None

    initial = tuple(jnp.zeros((TOKENS, FF), jnp.float32) for _ in range(3))
    totals, _ = lax.scan(scan_step, initial, jnp.arange(N_ROW, dtype=jnp.int32))
    return totals


def reference(tokens, grad_out, gate_weight, up_weight, down_weight):
    gate_sum, up_sum, grad_hidden = feature_block_sums(tokens, grad_out, gate_weight, up_weight, down_weight)
    sigmoid_gate = jax.nn.sigmoid(gate_sum)
    hidden = (gate_sum * sigmoid_gate * up_sum).astype(jnp.bfloat16)
    grad_up = (grad_hidden * gate_sum * sigmoid_gate).astype(jnp.bfloat16)
    grad_gate = (grad_hidden * up_sum * sigmoid_gate * (1.0 + gate_sum * (1.0 - sigmoid_gate))).astype(jnp.bfloat16)
    block_span = FF // N_COL

    def unit_step(running, block_index):
        offset = (block_index * block_span).astype(jnp.int32)
        gate_part = lax.dynamic_slice_in_dim(grad_gate, offset, block_span, 1)
        up_part = lax.dynamic_slice_in_dim(grad_up, offset, block_span, 1)
        gate_block = lax.dynamic_slice_in_dim(gate_weight, offset, block_span, 1)
        up_block = lax.dynamic_slice_in_dim(up_weight, offset, block_span, 1)
        contrib = jnp.dot(gate_part, gate_block.T, preferred_element_type=jnp.float32)
        contrib = contrib + jnp.dot(up_part, up_block.T, preferred_element_type=jnp.float32)
        rounded = lax.optimization_barrier(contrib.astype(jnp.bfloat16))
        return running + rounded.astype(jnp.float32), None

    grad_total, _ = lax.scan(unit_step, jnp.zeros((TOKENS, D), jnp.float32), jnp.arange(N_COL, dtype=jnp.int32))
    grad_tokens = grad_total.astype(jnp.bfloat16)
    grad_gate_weight = jnp.dot(tokens.T, grad_gate, preferred_element_type=jnp.float32).astype(jnp.bfloat16)
    grad_up_weight = jnp.dot(tokens.T, grad_up, preferred_element_type=jnp.float32).astype(jnp.bfloat16)
    grad_down_weight = jnp.dot(hidden.T, grad_out, preferred_element_type=jnp.float32).astype(jnp.bfloat16)
    return (grad_tokens, grad_gate_weight, grad_up_weight, grad_down_weight)
```

```python
import jax
import jax.numpy as jnp
from jax import lax
from jax.sharding import PartitionSpec as P


def contract_first(left, right):
    return lax.dot_general(
        left, right, (((0,), (0,)), ((), ())), preferred_element_type=jnp.float32
    )


def contract_last(left, right):
    return lax.dot_general(
        left, right, (((1,), (1,)), ((), ())), preferred_element_type=jnp.float32
    )


def gated_grads(gate_sum, up_sum, grad_hidden):
    sigmoid_gate = jax.nn.sigmoid(gate_sum)
    hidden = (gate_sum * sigmoid_gate * up_sum).astype(jnp.bfloat16)
    grad_up = (grad_hidden * gate_sum * sigmoid_gate).astype(jnp.bfloat16)
    grad_gate = (
        grad_hidden * up_sum * sigmoid_gate * (1.0 + gate_sum * (1.0 - sigmoid_gate))
    ).astype(jnp.bfloat16)
    return (hidden, grad_gate, grad_up)


def pick_chunks(units, wanted):
    for n in range(wanted, 0, -1):
        if units % n == 0 and (units // n) % 128 == 0:
            return n
    return 1


N_CHUNKS = 2


def body(tokens, grad_out, gate_weight, up_weight, down_weight):
    feat = tokens.shape[1]
    both = jnp.concatenate([tokens, grad_out], axis=1)
    both_all = lax.all_gather(both, "col", axis=0, tiled=True)
    tok_all = both_all[:, :feat]
    grad_all = both_all[:, feat:]
    tok_t = tok_all.T
    units = gate_weight.shape[1]
    n_chunks = pick_chunks(units, N_CHUNKS)
    span = units // n_chunks
    acc_gate, acc_up, acc_down = [], [], []
    partial_grad = None
    prev = None
    for k in range(n_chunks):
        lo = k * span
        gw = gate_weight[:, lo:lo + span]
        uw = up_weight[:, lo:lo + span]
        dw = down_weight[lo:lo + span, :]
        parts = (
            jnp.dot(tok_all, gw, preferred_element_type=jnp.float32).astype(jnp.bfloat16),
            jnp.dot(tok_all, uw, preferred_element_type=jnp.float32).astype(jnp.bfloat16),
            contract_last(grad_all, dw).astype(jnp.bfloat16),
        )
        if prev is not None:
            parts, _ = lax.optimization_barrier((parts, prev))
        sums = lax.psum(parts, "row")
        prev = sums
        gate_sum, up_sum, grad_hidden = (s.astype(jnp.float32) for s in sums)
        hidden, grad_gate, grad_up = gated_grads(gate_sum, up_sum, grad_hidden)
        acc_gate.append(jnp.dot(tok_t, grad_gate, preferred_element_type=jnp.float32).astype(jnp.bfloat16))
        acc_up.append(jnp.dot(tok_t, grad_up, preferred_element_type=jnp.float32).astype(jnp.bfloat16))
        acc_down.append(contract_first(hidden, grad_all).astype(jnp.bfloat16))
        part = contract_last(grad_gate, gw) + contract_last(grad_up, uw)
        partial_grad = part if partial_grad is None else partial_grad + part
    grad_tokens = lax.psum_scatter(
        partial_grad.astype(jnp.bfloat16), "col", scatter_dimension=0, tiled=True
    )
    return (
        grad_tokens,
        jnp.concatenate(acc_gate, axis=1),
        jnp.concatenate(acc_up, axis=1),
        jnp.concatenate(acc_down, axis=0),
    )


def solution(mesh):
    return jax.shard_map(
        body,
        mesh=mesh,
        in_specs=(
            P("col", "row"),
            P("col", "row"),
            P("row", "col"),
            P("row", "col"),
            P("col", "row"),
        ),
        out_specs=(P("col", "row"), P("row", "col"), P("row", "col"), P("col", "row")),
        check_vma=False,
    )
```

```python
import jax
import jax.numpy as jnp
from jax import lax
from jax.sharding import PartitionSpec as P


def contract_first(left, right):
    return lax.dot_general(
        left, right, (((0,), (0,)), ((), ())), preferred_element_type=jnp.float32
    )


def contract_last(left, right):
    return lax.dot_general(
        left, right, (((1,), (1,)), ((), ())), preferred_element_type=jnp.float32
    )


def gated_grads(gate_sum, up_sum, grad_hidden):
    sigmoid_gate = jax.nn.sigmoid(gate_sum)
    hidden = (gate_sum * sigmoid_gate * up_sum).astype(jnp.bfloat16)
    grad_up = (grad_hidden * gate_sum * sigmoid_gate).astype(jnp.bfloat16)
    grad_gate = (
        grad_hidden * up_sum * sigmoid_gate * (1.0 + gate_sum * (1.0 - sigmoid_gate))
    ).astype(jnp.bfloat16)
    return (hidden, grad_gate, grad_up)


def halving_reduce(parts, order, n_dev):
    r = lax.axis_index("row")
    cur = parts
    for step, bit in enumerate(order):
        n = cur[0].shape[0] // 2
        hi = (r // bit) % 2
        keep = tuple(lax.dynamic_slice_in_dim(c, hi * n, n, 0) for c in cur)
        send = tuple(lax.dynamic_slice_in_dim(c, (1 - hi) * n, n, 0) for c in cur)
        got = lax.ppermute(send, "row", [(j, j ^ bit) for j in range(n_dev)])
        summed = tuple(k.astype(jnp.float32) + g.astype(jnp.float32) for k, g in zip(keep, got))
        if step + 1 < len(order):
            summed = tuple(s.astype(jnp.bfloat16) for s in summed)
        cur = summed
    return cur


def doubling_gather(parts, order, n_dev):
    r = lax.axis_index("row")
    cur = parts
    for bit in reversed(order):
        n = cur[0].shape[0]
        hi = (r // bit) % 2
        got = lax.ppermute(cur, "row", [(j, j ^ bit) for j in range(n_dev)])
        nxt = []
        for c, g in zip(cur, got):
            out = jnp.zeros((2 * n,) + c.shape[1:], c.dtype)
            out = lax.dynamic_update_slice_in_dim(out, c, hi * n, 0)
            out = lax.dynamic_update_slice_in_dim(out, g, (1 - hi) * n, 0)
            nxt.append(out)
        cur = tuple(nxt)
    return cur


def row_bits(n_dev, tokens, units):
    if n_dev < 2 or n_dev & (n_dev - 1) or tokens % n_dev or units % 2:
        return None
    bits, b = [], 1
    while b < n_dev:
        bits.append(b)
        b *= 2
    return bits


def row_gated(gate_p, up_p, gh_p, n_dev):
    tokens, units = gate_p.shape
    bits = row_bits(n_dev, tokens, units)
    if bits is None:
        sums = lax.psum((gate_p, up_p, gh_p), "row")
        return gated_grads(*(s.astype(jnp.float32) for s in sums))
    orders = (bits, bits[:1] + bits[:0:-1])
    half = units // 2
    reduced = []
    for h, order in enumerate(orders):
        cols = tuple(a[:, h * half:(h + 1) * half] for a in (gate_p, up_p, gh_p))
        reduced.append(halving_reduce(cols, order, n_dev))
    outs = []
    for h, order in enumerate(orders):
        outs.append(doubling_gather(gated_grads(*reduced[h]), order, n_dev))
    return tuple(jnp.concatenate([outs[0][i], outs[1][i]], axis=1) for i in range(3))


def body(tokens, grad_out, gate_weight, up_weight, down_weight):
    n_row = lax.psum(1, "row")
    feat = tokens.shape[1]
    both = jnp.concatenate([tokens, grad_out], axis=1)
    both_all = lax.all_gather(both, "col", axis=0, tiled=True)
    tok_all = both_all[:, :feat]
    grad_all = both_all[:, feat:]
    tok_t = tok_all.T
    gate_p = jnp.dot(tok_all, gate_weight, preferred_element_type=jnp.float32).astype(jnp.bfloat16)
    up_p = jnp.dot(tok_all, up_weight, preferred_element_type=jnp.float32).astype(jnp.bfloat16)
    gh_p = contract_last(grad_all, down_weight).astype(jnp.bfloat16)
    hidden, grad_gate, grad_up = row_gated(gate_p, up_p, gh_p, n_row)
    acc_gate = jnp.dot(tok_t, grad_gate, preferred_element_type=jnp.float32)
    acc_up = jnp.dot(tok_t, grad_up, preferred_element_type=jnp.float32)
    acc_down = contract_first(hidden, grad_all)
    partial_grad = contract_last(grad_gate, gate_weight) + contract_last(grad_up, up_weight)
    grad_tokens = lax.psum_scatter(
        partial_grad.astype(jnp.bfloat16), "col", scatter_dimension=0, tiled=True
    )
    return (
        grad_tokens,
        acc_gate.astype(jnp.bfloat16),
        acc_up.astype(jnp.bfloat16),
        acc_down.astype(jnp.bfloat16),
    )


def solution(mesh):
    return jax.shard_map(
        body,
        mesh=mesh,
        in_specs=(
            P("col", "row"),
            P("col", "row"),
            P("row", "col"),
            P("row", "col"),
            P("col", "row"),
        ),
        out_specs=(P("col", "row"), P("row", "col"), P("row", "col"), P("col", "row")),
        check_vma=False,
    )
```

```python
import jax
import jax.numpy as jnp
from jax import lax
from jax.sharding import PartitionSpec as P


def contract_first(left, right):
    return lax.dot_general(
        left, right, (((0,), (0,)), ((), ())), preferred_element_type=jnp.float32
    )


def contract_last(left, right):
    return lax.dot_general(
        left, right, (((1,), (1,)), ((), ())), preferred_element_type=jnp.float32
    )


def gated_grads(gate_sum, up_sum, grad_hidden):
    sigmoid_gate = jax.nn.sigmoid(gate_sum)
    hidden = (gate_sum * sigmoid_gate * up_sum).astype(jnp.bfloat16)
    grad_up = (grad_hidden * gate_sum * sigmoid_gate).astype(jnp.bfloat16)
    grad_gate = (
        grad_hidden * up_sum * sigmoid_gate * (1.0 + gate_sum * (1.0 - sigmoid_gate))
    ).astype(jnp.bfloat16)
    return (hidden, grad_gate, grad_up)


def halving_reduce(parts, order, n_dev):
    cur = parts
    for step, bit in enumerate(order):
        n = cur[0].shape[0] // 2
        got = lax.ppermute(tuple(c[n:] for c in cur), "row", [(j, j ^ bit) for j in range(n_dev)])
        summed = tuple(c[:n].astype(jnp.float32) + g.astype(jnp.float32) for c, g in zip(cur, got))
        if step + 1 < len(order):
            summed = tuple(s.astype(jnp.bfloat16) for s in summed)
        cur = summed
    return cur


def doubling_gather(parts, order, n_dev):
    cur = parts
    for bit in reversed(order):
        got = lax.ppermute(cur, "row", [(j, j ^ bit) for j in range(n_dev)])
        cur = tuple(jnp.concatenate([c, g], axis=0) for c, g in zip(cur, got))
    return cur


def row_bits(n_dev, tokens, units):
    if n_dev < 2 or n_dev & (n_dev - 1) or tokens % n_dev or units % 2:
        return None
    bits, b = [], 1
    while b < n_dev:
        bits.append(b)
        b *= 2
    return bits


def block_mask(order):
    r = lax.axis_index("row")
    levels = len(order)
    mask = 0
    for k, bit in enumerate(order):
        mask = mask + ((r // bit) % 2) * (1 << (levels - 1 - k))
    return mask


def permute_blocks(x, n_dev, mask):
    idx = jnp.arange(n_dev, dtype=jnp.int32) ^ mask
    blocks = x.reshape((n_dev, x.shape[0] // n_dev) + x.shape[1:])
    return jnp.take(blocks, idx, axis=0).reshape(x.shape)


def body(tokens, grad_out, gate_weight, up_weight, down_weight):
    n_row = lax.psum(1, "row")
    feat = tokens.shape[1]
    both = jnp.concatenate([tokens, grad_out], axis=1)
    both_all = lax.all_gather(both, "col", axis=0, tiled=True)
    n_tok = both_all.shape[0]
    units = gate_weight.shape[1]
    bits = row_bits(n_row, n_tok, units)
    if bits is None:
        tok_all = both_all[:, :feat]
        grad_all = both_all[:, feat:]
        sums = lax.psum(
            (
                jnp.dot(tok_all, gate_weight, preferred_element_type=jnp.float32).astype(jnp.bfloat16),
                jnp.dot(tok_all, up_weight, preferred_element_type=jnp.float32).astype(jnp.bfloat16),
                contract_last(grad_all, down_weight).astype(jnp.bfloat16),
            ),
            "row",
        )
        hidden, grad_gate, grad_up = gated_grads(*(s.astype(jnp.float32) for s in sums))
        mask_a = None
    else:
        orders = (bits, bits[:1] + bits[:0:-1])
        masks = [block_mask(o) for o in orders]
        mask_a = masks[0]
        half = units // 2
        outs = []
        for h, order in enumerate(orders):
            both_h = permute_blocks(both_all, n_row, masks[h])
            tok_h = both_h[:, :feat]
            grad_h = both_h[:, feat:]
            cols = slice(h * half, (h + 1) * half)
            parts = (
                jnp.dot(tok_h, gate_weight[:, cols], preferred_element_type=jnp.float32).astype(jnp.bfloat16),
                jnp.dot(tok_h, up_weight[:, cols], preferred_element_type=jnp.float32).astype(jnp.bfloat16),
                contract_last(grad_h, down_weight[cols, :]).astype(jnp.bfloat16),
            )
            reduced = halving_reduce(parts, order, n_row)
            outs.append(doubling_gather(gated_grads(*reduced), order, n_row))
            if h == 0:
                tok_all, grad_all = tok_h, grad_h
        hidden, grad_gate, grad_up = (
            jnp.concatenate([outs[0][i], permute_blocks(outs[1][i], n_row, masks[0] ^ masks[1])], axis=1)
            for i in range(3)
        )
    tok_t = tok_all.T
    acc_gate = jnp.dot(tok_t, grad_gate, preferred_element_type=jnp.float32)
    acc_up = jnp.dot(tok_t, grad_up, preferred_element_type=jnp.float32)
    acc_down = contract_first(hidden, grad_all)
    partial_grad = contract_last(grad_gate, gate_weight) + contract_last(grad_up, up_weight)
    partial_grad = partial_grad.astype(jnp.bfloat16)
    if mask_a is not None:
        partial_grad = permute_blocks(partial_grad, n_row, mask_a)
    grad_tokens = lax.psum_scatter(partial_grad, "col", scatter_dimension=0, tiled=True)
    return (
        grad_tokens,
        acc_gate.astype(jnp.bfloat16),
        acc_up.astype(jnp.bfloat16),
        acc_down.astype(jnp.bfloat16),
    )


def solution(mesh):
    return jax.shard_map(
        body,
        mesh=mesh,
        in_specs=(
            P("col", "row"),
            P("col", "row"),
            P("row", "col"),
            P("row", "col"),
            P("col", "row"),
        ),
        out_specs=(P("col", "row"), P("row", "col"), P("row", "col"), P("col", "row")),
        check_vma=False,
    )
```

```python
import jax
import jax.numpy as jnp
from jax import lax
from jax.sharding import PartitionSpec as P


def contract_first(left, right):
    return lax.dot_general(
        left, right, (((0,), (0,)), ((), ())), preferred_element_type=jnp.float32
    )


def contract_last(left, right):
    return lax.dot_general(
        left, right, (((1,), (1,)), ((), ())), preferred_element_type=jnp.float32
    )


def gated_grads(gate_sum, up_sum, grad_hidden):
    sigmoid_gate = jax.nn.sigmoid(gate_sum)
    hidden = (gate_sum * sigmoid_gate * up_sum).astype(jnp.bfloat16)
    grad_up = (grad_hidden * gate_sum * sigmoid_gate).astype(jnp.bfloat16)
    grad_gate = (
        grad_hidden * up_sum * sigmoid_gate * (1.0 + gate_sum * (1.0 - sigmoid_gate))
    ).astype(jnp.bfloat16)
    return (hidden, grad_gate, grad_up)


def halving_reduce(x, order, n_dev):
    r = lax.axis_index("row")
    cur = x
    for step, bit in enumerate(order):
        n = cur.shape[1] // 2
        hi = (r // bit) % 2
        keep = lax.dynamic_slice_in_dim(cur, hi * n, n, 1)
        send = lax.dynamic_slice_in_dim(cur, (1 - hi) * n, n, 1)
        got = lax.ppermute(send, "row", [(j, j ^ bit) for j in range(n_dev)])
        cur = keep.astype(jnp.float32) + got.astype(jnp.float32)
        if step + 1 < len(order):
            cur = cur.astype(jnp.bfloat16)
    return cur


def doubling_gather(x, order, n_dev):
    r = lax.axis_index("row")
    cur = x
    for bit in reversed(order):
        hi = (r // bit) % 2
        got = lax.ppermute(cur, "row", [(j, j ^ bit) for j in range(n_dev)])
        cur = jnp.where(hi == 1, jnp.concatenate([got, cur], axis=1), jnp.concatenate([cur, got], axis=1))
    return cur


def row_bits(n_dev, tokens, units):
    if n_dev < 2 or n_dev & (n_dev - 1) or tokens % n_dev or units % 2:
        return None
    bits, b = [], 1
    while b < n_dev:
        bits.append(b)
        b *= 2
    return bits


def row_gated(stacked, n_dev):
    _, tokens, units = stacked.shape
    bits = row_bits(n_dev, tokens, units)
    if bits is None:
        sums = lax.psum(stacked, "row").astype(jnp.float32)
        return jnp.stack(gated_grads(sums[0], sums[1], sums[2]))
    orders = (bits, bits[:1] + bits[:0:-1])
    half = units // 2
    reduced = [halving_reduce(stacked[:, :, h * half:(h + 1) * half], o, n_dev) for h, o in enumerate(orders)]
    outs = [doubling_gather(jnp.stack(gated_grads(red[0], red[1], red[2])), o, n_dev) for red, o in zip(reduced, orders)]
    return jnp.concatenate(outs, axis=2)


def col_gather(x, n_col):
    parts = [x]
    for s in range(1, n_col):
        parts.append(lax.ppermute(x, "col", [(j, (j + s) % n_col) for j in range(n_col)]))
    return jnp.concatenate(parts, axis=0)


def col_reduce_scatter(x, n_col):
    span = x.shape[0] // n_col
    total = x[:span].astype(jnp.float32)
    for s in range(1, n_col):
        got = lax.ppermute(x[s * span:(s + 1) * span], "col", [(j, (j - s) % n_col) for j in range(n_col)])
        total = total + got.astype(jnp.float32)
    return total.astype(jnp.bfloat16)


def body(tokens, grad_out, gate_weight, up_weight, down_weight):
    n_row = lax.psum(1, "row")
    n_col = lax.psum(1, "col")
    tok_all = col_gather(tokens, n_col)
    grad_all = col_gather(grad_out, n_col)
    tok_t = tok_all.T
    stacked = jnp.stack(
        [
            jnp.dot(tok_all, gate_weight, preferred_element_type=jnp.float32).astype(jnp.bfloat16),
            jnp.dot(tok_all, up_weight, preferred_element_type=jnp.float32).astype(jnp.bfloat16),
            contract_last(grad_all, down_weight).astype(jnp.bfloat16),
        ]
    )
    gated = row_gated(stacked, n_row)
    hidden, grad_gate, grad_up = gated[0], gated[1], gated[2]
    partial_grad = contract_last(grad_gate, gate_weight) + contract_last(grad_up, up_weight)
    partial_grad, grad_gate, grad_up, hidden = lax.optimization_barrier(
        (partial_grad.astype(jnp.bfloat16), grad_gate, grad_up, hidden)
    )
    grad_tokens = col_reduce_scatter(partial_grad, n_col)
    acc_gate = jnp.dot(tok_t, grad_gate, preferred_element_type=jnp.float32)
    acc_up = jnp.dot(tok_t, grad_up, preferred_element_type=jnp.float32)
    acc_down = contract_first(hidden, grad_all)
    return (
        grad_tokens,
        acc_gate.astype(jnp.bfloat16),
        acc_up.astype(jnp.bfloat16),
        acc_down.astype(jnp.bfloat16),
    )


def solution(mesh):
    return jax.shard_map(
        body,
        mesh=mesh,
        in_specs=(
            P("col", "row"),
            P("col", "row"),
            P("row", "col"),
            P("row", "col"),
            P("col", "row"),
        ),
        out_specs=(P("col", "row"), P("row", "col"), P("row", "col"), P("col", "row")),
        check_vma=False,
    )
```

```python
import jax
import jax.numpy as jnp
from jax import lax
from jax.sharding import PartitionSpec as P


def contract_first(left, right):
    return lax.dot_general(
        left, right, (((0,), (0,)), ((), ())), preferred_element_type=jnp.float32
    )


def contract_last(left, right):
    return lax.dot_general(
        left, right, (((1,), (1,)), ((), ())), preferred_element_type=jnp.float32
    )


def gated_grads(gate_sum, up_sum, grad_hidden):
    sigmoid_gate = jax.nn.sigmoid(gate_sum)
    hidden = (gate_sum * sigmoid_gate * up_sum).astype(jnp.bfloat16)
    grad_up = (grad_hidden * gate_sum * sigmoid_gate).astype(jnp.bfloat16)
    grad_gate = (
        grad_hidden * up_sum * sigmoid_gate * (1.0 + gate_sum * (1.0 - sigmoid_gate))
    ).astype(jnp.bfloat16)
    return (hidden, grad_gate, grad_up)


def halving_reduce(x, order, n_dev):
    r = lax.axis_index("row")
    cur = x
    for step, bit in enumerate(order):
        n = cur.shape[1] // 2
        hi = (r // bit) % 2
        keep = lax.dynamic_slice_in_dim(cur, hi * n, n, 1)
        send = lax.dynamic_slice_in_dim(cur, (1 - hi) * n, n, 1)
        got = lax.ppermute(send, "row", [(j, j ^ bit) for j in range(n_dev)])
        cur = keep.astype(jnp.float32) + got.astype(jnp.float32)
        if step + 1 < len(order):
            cur = cur.astype(jnp.bfloat16)
    return cur


def doubling_gather(x, order, n_dev):
    r = lax.axis_index("row")
    cur = x
    for bit in reversed(order):
        hi = (r // bit) % 2
        got = lax.ppermute(cur, "row", [(j, j ^ bit) for j in range(n_dev)])
        cur = jnp.where(hi == 1, jnp.concatenate([got, cur], axis=1), jnp.concatenate([cur, got], axis=1))
    return cur


def row_bits(n_dev, tokens, units):
    if n_dev < 2 or n_dev & (n_dev - 1) or tokens % n_dev or units % 2:
        return None
    bits, b = [], 1
    while b < n_dev:
        bits.append(b)
        b *= 2
    return bits


def row_reduce(stacked, n_dev):
    _, tokens, units = stacked.shape
    bits = row_bits(n_dev, tokens, units)
    if bits is None:
        return (lax.psum(stacked, "row").astype(jnp.float32),)
    orders = (bits, bits[:1] + bits[:0:-1])
    half = units // 2
    return tuple(halving_reduce(stacked[:, :, h * half:(h + 1) * half], o, n_dev) for h, o in enumerate(orders))


def row_gather_gated(reduced, n_dev):
    if len(reduced) == 1:
        sums = reduced[0]
        return jnp.stack(gated_grads(sums[0], sums[1], sums[2]))
    bits = row_bits(n_dev, n_dev, 2)
    orders = (bits, bits[:1] + bits[:0:-1])
    outs = [doubling_gather(jnp.stack(gated_grads(red[0], red[1], red[2])), o, n_dev) for red, o in zip(reduced, orders)]
    return jnp.concatenate(outs, axis=2)


def col_gather(x, n_col):
    parts = [x]
    for s in range(1, n_col):
        parts.append(lax.ppermute(x, "col", [(j, (j + s) % n_col) for j in range(n_col)]))
    return jnp.concatenate(parts, axis=0)


def col_reduce_scatter(x, n_col):
    span = x.shape[0] // n_col
    total = x[:span].astype(jnp.float32)
    for s in range(1, n_col):
        got = lax.ppermute(x[s * span:(s + 1) * span], "col", [(j, (j - s) % n_col) for j in range(n_col)])
        total = total + got.astype(jnp.float32)
    return total.astype(jnp.bfloat16)


def pick_groups(units, wanted):
    for n in range(wanted, 0, -1):
        if units % (2 * n) == 0 and (units // (2 * n)) % 128 == 0:
            return n
    return 1


N_GROUPS = 2


def body(tokens, grad_out, gate_weight, up_weight, down_weight):
    n_row = lax.psum(1, "row")
    n_col = lax.psum(1, "col")
    tok_all = col_gather(tokens, n_col)
    grad_all = col_gather(grad_out, n_col)
    tok_t = tok_all.T
    units = gate_weight.shape[1]
    n_groups = pick_groups(units, N_GROUPS)
    span = units // n_groups
    hidden_g, grad_gate_g, grad_up_g = [], [], []
    for g in range(n_groups):
        cols = slice(g * span, (g + 1) * span)
        stacked = jnp.stack(
            [
                jnp.dot(tok_all, gate_weight[:, cols], preferred_element_type=jnp.float32).astype(jnp.bfloat16),
                jnp.dot(tok_all, up_weight[:, cols], preferred_element_type=jnp.float32).astype(jnp.bfloat16),
                contract_last(grad_all, down_weight[cols, :]).astype(jnp.bfloat16),
            ]
        )
        if g > 0:
            stacked, reduced = lax.optimization_barrier((stacked, reduced))
            gated = row_gather_gated(reduced, n_row)
            hidden_g.append(gated[0])
            grad_gate_g.append(gated[1])
            grad_up_g.append(gated[2])
        reduced = row_reduce(stacked, n_row)
    gated = row_gather_gated(reduced, n_row)
    hidden_g.append(gated[0])
    grad_gate_g.append(gated[1])
    grad_up_g.append(gated[2])
    partial_grad = None
    for g in range(n_groups):
        cols = slice(g * span, (g + 1) * span)
        part = contract_last(grad_gate_g[g], gate_weight[:, cols]) + contract_last(grad_up_g[g], up_weight[:, cols])
        partial_grad = part if partial_grad is None else partial_grad + part
    acc_down = jnp.concatenate(
        [contract_first(h, grad_all).astype(jnp.bfloat16) for h in hidden_g], axis=0
    )
    grad_gate = jnp.concatenate(grad_gate_g, axis=1)
    grad_up = jnp.concatenate(grad_up_g, axis=1)
    partial_grad, grad_gate, grad_up = lax.optimization_barrier(
        (partial_grad.astype(jnp.bfloat16), grad_gate, grad_up)
    )
    grad_tokens = col_reduce_scatter(partial_grad, n_col)
    acc_gate = jnp.dot(tok_t, grad_gate, preferred_element_type=jnp.float32)
    acc_up = jnp.dot(tok_t, grad_up, preferred_element_type=jnp.float32)
    return (
        grad_tokens,
        acc_gate.astype(jnp.bfloat16),
        acc_up.astype(jnp.bfloat16),
        acc_down,
    )


def solution(mesh):
    return jax.shard_map(
        body,
        mesh=mesh,
        in_specs=(
            P("col", "row"),
            P("col", "row"),
            P("row", "col"),
            P("row", "col"),
            P("col", "row"),
        ),
        out_specs=(P("col", "row"), P("row", "col"), P("row", "col"), P("col", "row")),
        check_vma=False,
    )
```

```python
import jax
import jax.numpy as jnp
from jax import lax
from jax.sharding import PartitionSpec as P


def contract_first(left, right):
    return lax.dot_general(
        left, right, (((0,), (0,)), ((), ())), preferred_element_type=jnp.float32
    )


def contract_last(left, right):
    return lax.dot_general(
        left, right, (((1,), (1,)), ((), ())), preferred_element_type=jnp.float32
    )


def gated_grads(gate_sum, up_sum, grad_hidden):
    sigmoid_gate = jax.nn.sigmoid(gate_sum)
    hidden = (gate_sum * sigmoid_gate * up_sum).astype(jnp.bfloat16)
    grad_up = (grad_hidden * gate_sum * sigmoid_gate).astype(jnp.bfloat16)
    grad_gate = (
        grad_hidden * up_sum * sigmoid_gate * (1.0 + gate_sum * (1.0 - sigmoid_gate))
    ).astype(jnp.bfloat16)
    return (hidden, grad_gate, grad_up)


def halving_reduce(x, order, n_dev):
    r = lax.axis_index("row")
    cur = x
    for step, bit in enumerate(order):
        n = cur.shape[1] // 2
        hi = (r // bit) % 2
        keep = lax.dynamic_slice_in_dim(cur, hi * n, n, 1)
        send = lax.dynamic_slice_in_dim(cur, (1 - hi) * n, n, 1)
        got = lax.ppermute(send, "row", [(j, j ^ bit) for j in range(n_dev)])
        cur = keep.astype(jnp.float32) + got.astype(jnp.float32)
        if step + 1 < len(order):
            cur = cur.astype(jnp.bfloat16)
    return cur


def doubling_gather(x, order, n_dev):
    r = lax.axis_index("row")
    cur = x
    for bit in reversed(order):
        hi = (r // bit) % 2
        got = lax.ppermute(cur, "row", [(j, j ^ bit) for j in range(n_dev)])
        cur = jnp.where(hi == 1, jnp.concatenate([got, cur], axis=1), jnp.concatenate([cur, got], axis=1))
    return cur


def row_bits(n_dev, tokens, units):
    if n_dev < 2 or n_dev & (n_dev - 1) or tokens % n_dev or units % 2:
        return None
    bits, b = [], 1
    while b < n_dev:
        bits.append(b)
        b *= 2
    return bits


def row_gated(stacked, n_dev):
    _, tokens, units = stacked.shape
    bits = row_bits(n_dev, tokens, units)
    if bits is None:
        sums = lax.psum(stacked, "row").astype(jnp.float32)
        return jnp.stack(gated_grads(sums[0], sums[1], sums[2]))
    orders = (bits, bits[:1] + bits[:0:-1])
    half = units // 2
    reduced = [halving_reduce(stacked[:, :, h * half:(h + 1) * half], o, n_dev) for h, o in enumerate(orders)]
    outs = [doubling_gather(jnp.stack(gated_grads(red[0], red[1], red[2])), o, n_dev) for red, o in zip(reduced, orders)]
    return jnp.concatenate(outs, axis=2)


def col_gather(x, n_col):
    parts = [x]
    for s in range(1, n_col):
        parts.append(lax.ppermute(x, "col", [(j, (j + s) % n_col) for j in range(n_col)]))
    return jnp.concatenate(parts, axis=0)


def col_reduce_scatter(x, n_col):
    span = x.shape[0] // n_col
    total = x[:span].astype(jnp.float32)
    for s in range(1, n_col):
        got = lax.ppermute(x[s * span:(s + 1) * span], "col", [(j, (j - s) % n_col) for j in range(n_col)])
        total = total + got.astype(jnp.float32)
    return total.astype(jnp.bfloat16)


def body(tokens, grad_out, gate_weight, up_weight, down_weight):
    n_row = lax.psum(1, "row")
    n_col = lax.psum(1, "col")
    tok_all = col_gather(tokens, n_col)
    grad_all = col_gather(grad_out, n_col)
    tok_t = tok_all.T
    stacked = jnp.stack(
        [
            jnp.dot(tok_all, gate_weight, preferred_element_type=jnp.float32).astype(jnp.bfloat16),
            jnp.dot(tok_all, up_weight, preferred_element_type=jnp.float32).astype(jnp.bfloat16),
            contract_last(grad_all, down_weight).astype(jnp.bfloat16),
        ]
    )
    gated = row_gated(stacked, n_row)
    hidden, grad_gate, grad_up = gated[0], gated[1], gated[2]
    partial_grad = contract_last(grad_gate, gate_weight) + contract_last(grad_up, up_weight)
    partial_grad, grad_gate, grad_up, hidden = lax.optimization_barrier(
        (partial_grad.astype(jnp.bfloat16), grad_gate, grad_up, hidden)
    )
    acc_gate = jnp.dot(tok_t, grad_gate, preferred_element_type=jnp.float32).astype(jnp.bfloat16)
    partial_grad, acc_gate, grad_up, hidden = lax.optimization_barrier((partial_grad, acc_gate, grad_up, hidden))
    grad_tokens = col_reduce_scatter(partial_grad, n_col)
    acc_up = jnp.dot(tok_t, grad_up, preferred_element_type=jnp.float32)
    acc_down = contract_first(hidden, grad_all)
    return (
        grad_tokens,
        acc_gate,
        acc_up.astype(jnp.bfloat16),
        acc_down.astype(jnp.bfloat16),
    )


def solution(mesh):
    return jax.shard_map(
        body,
        mesh=mesh,
        in_specs=(
            P("col", "row"),
            P("col", "row"),
            P("row", "col"),
            P("row", "col"),
            P("col", "row"),
        ),
        out_specs=(P("col", "row"), P("row", "col"), P("row", "col"), P("col", "row")),
        check_vma=False,
    )
```

```python
import jax
import jax.numpy as jnp
from jax import lax
from jax.sharding import PartitionSpec as P


def contract_first(left, right):
    return lax.dot_general(
        left, right, (((0,), (0,)), ((), ())), preferred_element_type=jnp.float32
    )


def contract_last(left, right):
    return lax.dot_general(
        left, right, (((1,), (1,)), ((), ())), preferred_element_type=jnp.float32
    )


def gated_grads(gate_sum, up_sum, grad_hidden):
    sigmoid_gate = jax.nn.sigmoid(gate_sum)
    hidden = (gate_sum * sigmoid_gate * up_sum).astype(jnp.bfloat16)
    grad_up = (grad_hidden * gate_sum * sigmoid_gate).astype(jnp.bfloat16)
    grad_gate = (
        grad_hidden * up_sum * sigmoid_gate * (1.0 + gate_sum * (1.0 - sigmoid_gate))
    ).astype(jnp.bfloat16)
    return (hidden, grad_gate, grad_up)


def halving_reduce(x, order, n_dev):
    r = lax.axis_index("row")
    cur = x
    for step, bit in enumerate(order):
        n = cur.shape[1] // 2
        hi = (r // bit) % 2
        keep = lax.dynamic_slice_in_dim(cur, hi * n, n, 1)
        send = lax.dynamic_slice_in_dim(cur, (1 - hi) * n, n, 1)
        got = lax.ppermute(send, "row", [(j, j ^ bit) for j in range(n_dev)])
        cur = keep.astype(jnp.float32) + got.astype(jnp.float32)
        if step + 1 < len(order):
            cur = cur.astype(jnp.bfloat16)
    return cur


def doubling_gather(x, order, n_dev):
    r = lax.axis_index("row")
    cur = x
    for bit in reversed(order):
        hi = (r // bit) % 2
        got = lax.ppermute(cur, "row", [(j, j ^ bit) for j in range(n_dev)])
        cur = jnp.where(hi == 1, jnp.concatenate([got, cur], axis=1), jnp.concatenate([cur, got], axis=1))
    return cur


def row_bits(n_dev, tokens, units):
    if n_dev < 2 or n_dev & (n_dev - 1) or tokens % n_dev or units % 2:
        return None
    bits, b = [], 1
    while b < n_dev:
        bits.append(b)
        b *= 2
    return bits


def row_gated(stacked, n_dev):
    _, tokens, units = stacked.shape
    bits = row_bits(n_dev, tokens, units)
    if bits is None:
        sums = lax.psum(stacked, "row").astype(jnp.float32)
        return jnp.stack(gated_grads(sums[0], sums[1], sums[2]))
    orders = (bits, bits[:1] + bits[:0:-1])
    half = units // 2
    reduced = [halving_reduce(stacked[:, :, h * half:(h + 1) * half], o, n_dev) for h, o in enumerate(orders)]
    outs = [doubling_gather(jnp.stack(gated_grads(red[0], red[1], red[2])), o, n_dev) for red, o in zip(reduced, orders)]
    return jnp.concatenate(outs, axis=2)


def col_gather(x, n_col):
    parts = [x]
    for s in range(1, n_col):
        parts.append(lax.ppermute(x, "col", [(j, (j + s) % n_col) for j in range(n_col)]))
    return jnp.concatenate(parts, axis=0)


def col_reduce_scatter(x, n_col):
    span = x.shape[0] // n_col
    total = x[:span].astype(jnp.float32)
    for s in range(1, n_col):
        got = lax.ppermute(x[s * span:(s + 1) * span], "col", [(j, (j - s) % n_col) for j in range(n_col)])
        total = total + got.astype(jnp.float32)
    return total.astype(jnp.bfloat16)


def body(tokens, grad_out, gate_weight, up_weight, down_weight):
    n_row = lax.psum(1, "row")
    n_col = lax.psum(1, "col")
    feat = tokens.shape[1]
    both_all = col_gather(jnp.concatenate([tokens, grad_out], axis=1), n_col)
    tok_all = both_all[:, :feat]
    grad_all = both_all[:, feat:]
    tok_t = tok_all.T
    stacked = jnp.stack(
        [
            jnp.dot(tok_all, gate_weight, preferred_element_type=jnp.float32).astype(jnp.bfloat16),
            jnp.dot(tok_all, up_weight, preferred_element_type=jnp.float32).astype(jnp.bfloat16),
            contract_last(grad_all, down_weight).astype(jnp.bfloat16),
        ]
    )
    gated = row_gated(stacked, n_row)
    hidden, grad_gate, grad_up = gated[0], gated[1], gated[2]
    partial_grad = contract_last(grad_gate, gate_weight) + contract_last(grad_up, up_weight)
    partial_grad, grad_gate, grad_up, hidden = lax.optimization_barrier(
        (partial_grad.astype(jnp.bfloat16), grad_gate, grad_up, hidden)
    )
    acc_gate = jnp.dot(tok_t, grad_gate, preferred_element_type=jnp.float32).astype(jnp.bfloat16)
    partial_grad, acc_gate, grad_up, hidden = lax.optimization_barrier((partial_grad, acc_gate, grad_up, hidden))
    grad_tokens = col_reduce_scatter(partial_grad, n_col)
    acc_up = jnp.dot(tok_t, grad_up, preferred_element_type=jnp.float32)
    acc_down = contract_first(hidden, grad_all)
    return (
        grad_tokens,
        acc_gate,
        acc_up.astype(jnp.bfloat16),
        acc_down.astype(jnp.bfloat16),
    )


def solution(mesh):
    return jax.shard_map(
        body,
        mesh=mesh,
        in_specs=(
            P("col", "row"),
            P("col", "row"),
            P("row", "col"),
            P("row", "col"),
            P("col", "row"),
        ),
        out_specs=(P("col", "row"), P("row", "col"), P("row", "col"), P("col", "row")),
        check_vma=False,
    )
```

```python
import jax
import jax.numpy as jnp
from jax import lax
from jax.sharding import PartitionSpec as P


def contract_first(left, right):
    return lax.dot_general(
        left, right, (((0,), (0,)), ((), ())), preferred_element_type=jnp.float32
    )


def contract_last(left, right):
    return lax.dot_general(
        left, right, (((1,), (1,)), ((), ())), preferred_element_type=jnp.float32
    )


def gated_grads(gate_sum, up_sum, grad_hidden):
    sigmoid_gate = jax.nn.sigmoid(gate_sum)
    hidden = (gate_sum * sigmoid_gate * up_sum).astype(jnp.bfloat16)
    grad_up = (grad_hidden * gate_sum * sigmoid_gate).astype(jnp.bfloat16)
    grad_gate = (
        grad_hidden * up_sum * sigmoid_gate * (1.0 + gate_sum * (1.0 - sigmoid_gate))
    ).astype(jnp.bfloat16)
    return (hidden, grad_gate, grad_up)


def halving_reduce(x, order, n_dev):
    r = lax.axis_index("row")
    cur = x
    for step, bit in enumerate(order):
        n = cur.shape[1] // 2
        hi = (r // bit) % 2
        keep = lax.dynamic_slice_in_dim(cur, hi * n, n, 1)
        send = lax.dynamic_slice_in_dim(cur, (1 - hi) * n, n, 1)
        got = lax.ppermute(send, "row", [(j, j ^ bit) for j in range(n_dev)])
        cur = keep.astype(jnp.float32) + got.astype(jnp.float32)
        if step + 1 < len(order):
            cur = cur.astype(jnp.bfloat16)
    return cur


def doubling_gather(x, order, n_dev):
    r = lax.axis_index("row")
    cur = x
    for bit in reversed(order):
        hi = (r // bit) % 2
        got = lax.ppermute(cur, "row", [(j, j ^ bit) for j in range(n_dev)])
        cur = jnp.where(hi == 1, jnp.concatenate([got, cur], axis=1), jnp.concatenate([cur, got], axis=1))
    return cur


def row_bits(n_dev, tokens, units):
    if n_dev < 2 or n_dev & (n_dev - 1) or tokens % n_dev or units % 2:
        return None
    bits, b = [], 1
    while b < n_dev:
        bits.append(b)
        b *= 2
    return bits


def row_reduce(stacked, n_dev):
    _, tokens, units = stacked.shape
    bits = row_bits(n_dev, tokens, units)
    if bits is None:
        return (lax.psum(stacked, "row").astype(jnp.float32),)
    orders = (bits, bits[:1] + bits[:0:-1])
    half = units // 2
    return tuple(halving_reduce(stacked[:, :, h * half:(h + 1) * half], o, n_dev) for h, o in enumerate(orders))


def row_gather_gated(reduced, n_dev):
    if len(reduced) == 1:
        sums = reduced[0]
        return jnp.stack(gated_grads(sums[0], sums[1], sums[2]))
    bits = row_bits(n_dev, n_dev, 2)
    orders = (bits, bits[:1] + bits[:0:-1])
    outs = [doubling_gather(jnp.stack(gated_grads(red[0], red[1], red[2])), o, n_dev) for red, o in zip(reduced, orders)]
    return jnp.concatenate(outs, axis=2)


def col_gather(x, n_col):
    parts = [x]
    for s in range(1, n_col):
        parts.append(lax.ppermute(x, "col", [(j, (j + s) % n_col) for j in range(n_col)]))
    return jnp.concatenate(parts, axis=0)


def col_reduce_scatter(x, n_col):
    span = x.shape[0] // n_col
    total = x[:span].astype(jnp.float32)
    for s in range(1, n_col):
        got = lax.ppermute(x[s * span:(s + 1) * span], "col", [(j, (j - s) % n_col) for j in range(n_col)])
        total = total + got.astype(jnp.float32)
    return total.astype(jnp.bfloat16)


def col_gather_remote(x, n_col):
    return [lax.ppermute(x, "col", [(j, (j + s) % n_col) for j in range(n_col)]) for s in range(1, n_col)]


def body(tokens, grad_out, gate_weight, up_weight, down_weight):
    n_row = lax.psum(1, "row")
    n_col = lax.psum(1, "col")
    feat = tokens.shape[1]
    n_own = tokens.shape[0]
    units = gate_weight.shape[1]
    both = jnp.concatenate([tokens, grad_out], axis=1)
    staged = (
        n_col > 1
        and row_bits(n_row, n_own, units) is not None
        and (n_own * (n_col - 1)) % n_row == 0
    )
    if staged:
        stages = [both, col_gather_remote(both, n_col)]
    else:
        stages = [col_gather(both, n_col)]
    gated_parts = []
    reduced = None
    for i, st in enumerate(stages):
        if i > 0:
            st, reduced = lax.optimization_barrier((st, reduced))
            st = jnp.concatenate(st, axis=0)
            stages[i] = st
            gated_parts.append(row_gather_gated(reduced, n_row))
        tok_s = st[:, :feat]
        grad_s = st[:, feat:]
        stacked = jnp.stack(
            [
                jnp.dot(tok_s, gate_weight, preferred_element_type=jnp.float32).astype(jnp.bfloat16),
                jnp.dot(tok_s, up_weight, preferred_element_type=jnp.float32).astype(jnp.bfloat16),
                contract_last(grad_s, down_weight).astype(jnp.bfloat16),
            ]
        )
        reduced = row_reduce(stacked, n_row)
    gated_parts.append(row_gather_gated(reduced, n_row))
    gated = jnp.concatenate(gated_parts, axis=1) if len(gated_parts) > 1 else gated_parts[0]
    both_all = jnp.concatenate(stages, axis=0) if len(stages) > 1 else stages[0]
    tok_all = both_all[:, :feat]
    grad_all = both_all[:, feat:]
    tok_t = tok_all.T
    hidden, grad_gate, grad_up = gated[0], gated[1], gated[2]
    partial_grad = contract_last(grad_gate, gate_weight) + contract_last(grad_up, up_weight)
    partial_grad, grad_gate, grad_up, hidden = lax.optimization_barrier(
        (partial_grad.astype(jnp.bfloat16), grad_gate, grad_up, hidden)
    )
    acc_gate = jnp.dot(tok_t, grad_gate, preferred_element_type=jnp.float32).astype(jnp.bfloat16)
    partial_grad, acc_gate, grad_up, hidden = lax.optimization_barrier((partial_grad, acc_gate, grad_up, hidden))
    grad_tokens = col_reduce_scatter(partial_grad, n_col)
    acc_up = jnp.dot(tok_t, grad_up, preferred_element_type=jnp.float32)
    acc_down = contract_first(hidden, grad_all)
    return (
        grad_tokens,
        acc_gate,
        acc_up.astype(jnp.bfloat16),
        acc_down.astype(jnp.bfloat16),
    )


def solution(mesh):
    return jax.shard_map(
        body,
        mesh=mesh,
        in_specs=(
            P("col", "row"),
            P("col", "row"),
            P("row", "col"),
            P("row", "col"),
            P("col", "row"),
        ),
        out_specs=(P("col", "row"), P("row", "col"), P("row", "col"), P("col", "row")),
        check_vma=False,
    )
```

```python
import jax
import jax.numpy as jnp
from jax import lax
from jax.sharding import PartitionSpec as P


def contract_first(left, right):
    return lax.dot_general(
        left, right, (((0,), (0,)), ((), ())), preferred_element_type=jnp.float32
    )


def contract_last(left, right):
    return lax.dot_general(
        left, right, (((1,), (1,)), ((), ())), preferred_element_type=jnp.float32
    )


def gated_grads(gate_sum, up_sum, grad_hidden):
    sigmoid_gate = jax.nn.sigmoid(gate_sum)
    hidden = (gate_sum * sigmoid_gate * up_sum).astype(jnp.bfloat16)
    grad_up = (grad_hidden * gate_sum * sigmoid_gate).astype(jnp.bfloat16)
    grad_gate = (
        grad_hidden * up_sum * sigmoid_gate * (1.0 + gate_sum * (1.0 - sigmoid_gate))
    ).astype(jnp.bfloat16)
    return (hidden, grad_gate, grad_up)


def halving_reduce(x, order, n_dev):
    r = lax.axis_index("row")
    cur = x
    for step, bit in enumerate(order):
        n = cur.shape[1] // 2
        hi = (r // bit) % 2
        keep = lax.dynamic_slice_in_dim(cur, hi * n, n, 1)
        send = lax.dynamic_slice_in_dim(cur, (1 - hi) * n, n, 1)
        got = lax.ppermute(send, "row", [(j, j ^ bit) for j in range(n_dev)])
        cur = keep.astype(jnp.float32) + got.astype(jnp.float32)
        if step + 1 < len(order):
            cur = cur.astype(jnp.bfloat16)
    return cur


def doubling_gather(x, order, n_dev):
    r = lax.axis_index("row")
    cur = x
    for bit in reversed(order):
        hi = (r // bit) % 2
        got = lax.ppermute(cur, "row", [(j, j ^ bit) for j in range(n_dev)])
        cur = jnp.where(hi == 1, jnp.concatenate([got, cur], axis=1), jnp.concatenate([cur, got], axis=1))
    return cur


def row_bits(n_dev, tokens, units):
    if n_dev < 2 or n_dev & (n_dev - 1) or tokens % n_dev or units % 2:
        return None
    bits, b = [], 1
    while b < n_dev:
        bits.append(b)
        b *= 2
    return bits


def row_reduce(stacked, n_dev):
    _, tokens, units = stacked.shape
    bits = row_bits(n_dev, tokens, units)
    if bits is None:
        return (lax.psum(stacked, "row").astype(jnp.float32),)
    orders = (bits, bits[:1] + bits[:0:-1])
    half = units // 2
    return tuple(halving_reduce(stacked[:, :, h * half:(h + 1) * half], o, n_dev) for h, o in enumerate(orders))


def row_gather_gated(reduced, n_dev):
    if len(reduced) == 1:
        sums = reduced[0]
        return jnp.stack(gated_grads(sums[0], sums[1], sums[2]))
    bits = row_bits(n_dev, n_dev, 2)
    orders = (bits, bits[:1] + bits[:0:-1])
    outs = [doubling_gather(jnp.stack(gated_grads(red[0], red[1], red[2])), o, n_dev) for red, o in zip(reduced, orders)]
    return jnp.concatenate(outs, axis=2)


def col_gather(x, n_col):
    parts = [x]
    for s in range(1, n_col):
        parts.append(lax.ppermute(x, "col", [(j, (j + s) % n_col) for j in range(n_col)]))
    return jnp.concatenate(parts, axis=0)


def col_reduce_scatter(x, n_col):
    span = x.shape[0] // n_col
    total = x[:span].astype(jnp.float32)
    for s in range(1, n_col):
        got = lax.ppermute(x[s * span:(s + 1) * span], "col", [(j, (j - s) % n_col) for j in range(n_col)])
        total = total + got.astype(jnp.float32)
    return total.astype(jnp.bfloat16)


def col_gather_remote(x, n_col):
    return [lax.ppermute(x, "col", [(j, (j + s) % n_col) for j in range(n_col)]) for s in range(1, n_col)]


def body(tokens, grad_out, gate_weight, up_weight, down_weight):
    n_row = lax.psum(1, "row")
    n_col = lax.psum(1, "col")
    feat = tokens.shape[1]
    n_own = tokens.shape[0]
    units = gate_weight.shape[1]
    both = jnp.concatenate([tokens, grad_out], axis=1)
    staged = (
        n_col > 1
        and row_bits(n_row, n_own, units) is not None
        and (n_own * (n_col - 1)) % n_row == 0
    )
    if staged:
        stages = [both, col_gather_remote(both, n_col)]
    else:
        stages = [col_gather(both, n_col)]
    if staged:
        stages[1] = jnp.concatenate(stages[1], axis=0)
    gated_parts = []
    for st in stages:
        tok_s = st[:, :feat]
        grad_s = st[:, feat:]
        stacked = jnp.stack(
            [
                jnp.dot(tok_s, gate_weight, preferred_element_type=jnp.float32).astype(jnp.bfloat16),
                jnp.dot(tok_s, up_weight, preferred_element_type=jnp.float32).astype(jnp.bfloat16),
                contract_last(grad_s, down_weight).astype(jnp.bfloat16),
            ]
        )
        gated_parts.append(row_gather_gated(row_reduce(stacked, n_row), n_row))
    gated = jnp.concatenate(gated_parts, axis=1) if len(gated_parts) > 1 else gated_parts[0]
    both_all = jnp.concatenate(stages, axis=0) if len(stages) > 1 else stages[0]
    tok_all = both_all[:, :feat]
    grad_all = both_all[:, feat:]
    tok_t = tok_all.T
    hidden, grad_gate, grad_up = gated[0], gated[1], gated[2]
    partial_grad = contract_last(grad_gate, gate_weight) + contract_last(grad_up, up_weight)
    partial_grad, grad_gate, grad_up, hidden = lax.optimization_barrier(
        (partial_grad.astype(jnp.bfloat16), grad_gate, grad_up, hidden)
    )
    acc_gate = jnp.dot(tok_t, grad_gate, preferred_element_type=jnp.float32).astype(jnp.bfloat16)
    partial_grad, acc_gate, grad_up, hidden = lax.optimization_barrier((partial_grad, acc_gate, grad_up, hidden))
    grad_tokens = col_reduce_scatter(partial_grad, n_col)
    acc_up = jnp.dot(tok_t, grad_up, preferred_element_type=jnp.float32)
    acc_down = contract_first(hidden, grad_all)
    return (
        grad_tokens,
        acc_gate,
        acc_up.astype(jnp.bfloat16),
        acc_down.astype(jnp.bfloat16),
    )


def solution(mesh):
    return jax.shard_map(
        body,
        mesh=mesh,
        in_specs=(
            P("col", "row"),
            P("col", "row"),
            P("row", "col"),
            P("row", "col"),
            P("col", "row"),
        ),
        out_specs=(P("col", "row"), P("row", "col"), P("row", "col"), P("col", "row")),
        check_vma=False,
    )
```

```python
import jax
import jax.numpy as jnp
from jax import lax
from jax.sharding import PartitionSpec as P


def contract_first(left, right):
    return lax.dot_general(
        left, right, (((0,), (0,)), ((), ())), preferred_element_type=jnp.float32
    )


def contract_last(left, right):
    return lax.dot_general(
        left, right, (((1,), (1,)), ((), ())), preferred_element_type=jnp.float32
    )


def gated_grads(gate_sum, up_sum, grad_hidden):
    sigmoid_gate = jax.nn.sigmoid(gate_sum)
    hidden = (gate_sum * sigmoid_gate * up_sum).astype(jnp.bfloat16)
    grad_up = (grad_hidden * gate_sum * sigmoid_gate).astype(jnp.bfloat16)
    grad_gate = (
        grad_hidden * up_sum * sigmoid_gate * (1.0 + gate_sum * (1.0 - sigmoid_gate))
    ).astype(jnp.bfloat16)
    return (hidden, grad_gate, grad_up)


def halving_reduce(x, order, n_dev):
    r = lax.axis_index("row")
    cur = x
    for step, bit in enumerate(order):
        n = cur.shape[1] // 2
        hi = (r // bit) % 2
        keep = lax.dynamic_slice_in_dim(cur, hi * n, n, 1)
        send = lax.dynamic_slice_in_dim(cur, (1 - hi) * n, n, 1)
        got = lax.ppermute(send, "row", [(j, j ^ bit) for j in range(n_dev)])
        cur = keep.astype(jnp.float32) + got.astype(jnp.float32)
        if step + 1 < len(order):
            cur = cur.astype(jnp.bfloat16)
    return cur


def doubling_gather(x, order, n_dev):
    r = lax.axis_index("row")
    cur = x
    for bit in reversed(order):
        hi = (r // bit) % 2
        got = lax.ppermute(cur, "row", [(j, j ^ bit) for j in range(n_dev)])
        cur = jnp.where(hi == 1, jnp.concatenate([got, cur], axis=1), jnp.concatenate([cur, got], axis=1))
    return cur


def row_bits(n_dev, tokens, units):
    if n_dev < 2 or n_dev & (n_dev - 1) or tokens % n_dev or units % N_PARTS:
        return None
    bits, b = [], 1
    while b < n_dev:
        bits.append(b)
        b *= 2
    return bits


def row_gated(stacked, n_dev):
    _, tokens, units = stacked.shape
    bits = row_bits(n_dev, tokens, units)
    if bits is None:
        sums = lax.psum(stacked, "row").astype(jnp.float32)
        return jnp.stack(gated_grads(sums[0], sums[1], sums[2]))
    orders = (bits, bits[:1] + bits[:0:-1]) * (N_PARTS // 2)
    span = units // len(orders)
    reduced = [halving_reduce(stacked[:, :, h * span:(h + 1) * span], o, n_dev) for h, o in enumerate(orders)]
    outs = [doubling_gather(jnp.stack(gated_grads(red[0], red[1], red[2])), o, n_dev) for red, o in zip(reduced, orders)]
    return jnp.concatenate(outs, axis=2)


N_PARTS = 4


def col_gather(x, n_col):
    parts = [x]
    for s in range(1, n_col):
        parts.append(lax.ppermute(x, "col", [(j, (j + s) % n_col) for j in range(n_col)]))
    return jnp.concatenate(parts, axis=0)


def col_reduce_scatter(x, n_col):
    span = x.shape[0] // n_col
    total = x[:span].astype(jnp.float32)
    for s in range(1, n_col):
        got = lax.ppermute(x[s * span:(s + 1) * span], "col", [(j, (j - s) % n_col) for j in range(n_col)])
        total = total + got.astype(jnp.float32)
    return total.astype(jnp.bfloat16)


def body(tokens, grad_out, gate_weight, up_weight, down_weight):
    n_row = lax.psum(1, "row")
    n_col = lax.psum(1, "col")
    tok_all = col_gather(tokens, n_col)
    grad_all = col_gather(grad_out, n_col)
    tok_t = tok_all.T
    stacked = jnp.stack(
        [
            jnp.dot(tok_all, gate_weight, preferred_element_type=jnp.float32).astype(jnp.bfloat16),
            jnp.dot(tok_all, up_weight, preferred_element_type=jnp.float32).astype(jnp.bfloat16),
            contract_last(grad_all, down_weight).astype(jnp.bfloat16),
        ]
    )
    gated = row_gated(stacked, n_row)
    hidden, grad_gate, grad_up = gated[0], gated[1], gated[2]
    partial_grad = contract_last(grad_gate, gate_weight) + contract_last(grad_up, up_weight)
    partial_grad, grad_gate, grad_up, hidden = lax.optimization_barrier(
        (partial_grad.astype(jnp.bfloat16), grad_gate, grad_up, hidden)
    )
    acc_gate = jnp.dot(tok_t, grad_gate, preferred_element_type=jnp.float32).astype(jnp.bfloat16)
    partial_grad, acc_gate, grad_up, hidden = lax.optimization_barrier((partial_grad, acc_gate, grad_up, hidden))
    grad_tokens = col_reduce_scatter(partial_grad, n_col)
    acc_up = jnp.dot(tok_t, grad_up, preferred_element_type=jnp.float32)
    acc_down = contract_first(hidden, grad_all)
    return (
        grad_tokens,
        acc_gate,
        acc_up.astype(jnp.bfloat16),
        acc_down.astype(jnp.bfloat16),
    )


def solution(mesh):
    return jax.shard_map(
        body,
        mesh=mesh,
        in_specs=(
            P("col", "row"),
            P("col", "row"),
            P("row", "col"),
            P("row", "col"),
            P("col", "row"),
        ),
        out_specs=(P("col", "row"), P("row", "col"), P("row", "col"), P("col", "row")),
        check_vma=False,
    )
```

```python
import jax
import jax.numpy as jnp
from jax import lax
from jax.sharding import PartitionSpec as P


def contract_first(left, right):
    return lax.dot_general(
        left, right, (((0,), (0,)), ((), ())), preferred_element_type=jnp.float32
    )


def contract_last(left, right):
    return lax.dot_general(
        left, right, (((1,), (1,)), ((), ())), preferred_element_type=jnp.float32
    )


def gated_grads(gate_sum, up_sum, grad_hidden):
    sigmoid_gate = jax.nn.sigmoid(gate_sum)
    hidden = (gate_sum * sigmoid_gate * up_sum).astype(jnp.bfloat16)
    grad_up = (grad_hidden * gate_sum * sigmoid_gate).astype(jnp.bfloat16)
    grad_gate = (
        grad_hidden * up_sum * sigmoid_gate * (1.0 + gate_sum * (1.0 - sigmoid_gate))
    ).astype(jnp.bfloat16)
    return (hidden, grad_gate, grad_up)


def halving_reduce(x, order, n_dev):
    r = lax.axis_index("row")
    cur = x
    for step, bit in enumerate(order):
        n = cur.shape[1] // 2
        hi = (r // bit) % 2
        keep = lax.dynamic_slice_in_dim(cur, hi * n, n, 1)
        send = lax.dynamic_slice_in_dim(cur, (1 - hi) * n, n, 1)
        got = lax.ppermute(send, "row", [(j, j ^ bit) for j in range(n_dev)])
        cur = keep.astype(jnp.float32) + got.astype(jnp.float32)
        if step + 1 < len(order):
            cur = cur.astype(jnp.bfloat16)
    return cur


def doubling_gather(x, order, n_dev):
    r = lax.axis_index("row")
    cur = x
    for bit in reversed(order):
        hi = (r // bit) % 2
        got = lax.ppermute(cur, "row", [(j, j ^ bit) for j in range(n_dev)])
        cur = jnp.where(hi == 1, jnp.concatenate([got, cur], axis=1), jnp.concatenate([cur, got], axis=1))
    return cur


def row_bits(n_dev, tokens, units):
    if n_dev < 2 or n_dev & (n_dev - 1) or tokens % n_dev or units % 2:
        return None
    bits, b = [], 1
    while b < n_dev:
        bits.append(b)
        b *= 2
    return bits


def row_gated(stacked, n_dev):
    _, tokens, units = stacked.shape
    bits = row_bits(n_dev, tokens, units)
    if bits is None:
        sums = lax.psum(stacked, "row").astype(jnp.float32)
        return jnp.stack(gated_grads(sums[0], sums[1], sums[2]))
    orders = (bits, bits[:1] + bits[:0:-1])
    half = units // 2
    reduced = [halving_reduce(stacked[:, :, h * half:(h + 1) * half], o, n_dev) for h, o in enumerate(orders)]
    outs = [doubling_gather(jnp.stack(gated_grads(red[0], red[1], red[2])), o, n_dev) for red, o in zip(reduced, orders)]
    return jnp.concatenate(outs, axis=2)


def col_gather(x, n_col):
    parts = [x]
    for s in range(1, n_col):
        parts.append(lax.ppermute(x, "col", [(j, (j + s) % n_col) for j in range(n_col)]))
    return jnp.concatenate(parts, axis=0)


def col_reduce_scatter(x, n_col):
    span = x.shape[0] // n_col
    total = x[:span].astype(jnp.float32)
    for s in range(1, n_col):
        got = lax.ppermute(x[s * span:(s + 1) * span], "col", [(j, (j - s) % n_col) for j in range(n_col)])
        total = total + got.astype(jnp.float32)
    return total.astype(jnp.bfloat16)


def body(tokens, grad_out, gate_weight, up_weight, down_weight):
    n_row = lax.psum(1, "row")
    n_col = lax.psum(1, "col")
    tok_all = col_gather(tokens, n_col)
    grad_all = col_gather(grad_out, n_col)
    tok_t = tok_all.T
    stacked = jnp.stack(
        [
            jnp.dot(tok_all, gate_weight, preferred_element_type=jnp.float32).astype(jnp.bfloat16),
            jnp.dot(tok_all, up_weight, preferred_element_type=jnp.float32).astype(jnp.bfloat16),
            contract_last(grad_all, down_weight).astype(jnp.bfloat16),
        ]
    )
    gated = row_gated(stacked, n_row)
    hidden, grad_gate, grad_up = gated[0], gated[1], gated[2]
    partial_grad = contract_last(grad_gate, gate_weight) + contract_last(grad_up, up_weight)
    partial_grad, grad_gate, grad_up, hidden = lax.optimization_barrier(
        (partial_grad.astype(jnp.bfloat16), grad_gate, grad_up, hidden)
    )
    span = partial_grad.shape[0] // n_col
    shifts = list(range(1, n_col))
    groups = [shifts[i::3] for i in range(3)]
    total = partial_grad[:span].astype(jnp.float32)
    received = []
    weights = []
    for i, (lhs, rhs, first) in enumerate(((tok_t, grad_gate, False), (tok_t, grad_up, False), (hidden, grad_all, True))):
        for s in groups[i]:
            received.append(
                lax.ppermute(partial_grad[s * span:(s + 1) * span], "col", [(j, (j - s) % n_col) for j in range(n_col)])
            )
        if first:
            acc = contract_first(lhs, rhs)
        else:
            acc = jnp.dot(lhs, rhs, preferred_element_type=jnp.float32)
        acc = acc.astype(jnp.bfloat16)
        if i < 2:
            acc, partial_grad = lax.optimization_barrier((acc, partial_grad))
        weights.append(acc)
    for got in received:
        total = total + got.astype(jnp.float32)
    grad_tokens = total.astype(jnp.bfloat16)
    acc_gate, acc_up, acc_down = weights
    return (
        grad_tokens,
        acc_gate,
        acc_up,
        acc_down,
    )


def solution(mesh):
    return jax.shard_map(
        body,
        mesh=mesh,
        in_specs=(
            P("col", "row"),
            P("col", "row"),
            P("row", "col"),
            P("row", "col"),
            P("col", "row"),
        ),
        out_specs=(P("col", "row"), P("row", "col"), P("row", "col"), P("col", "row")),
        check_vma=False,
    )
```

```python
import jax
import jax.numpy as jnp
from jax import lax
from jax.sharding import PartitionSpec as P


def contract_first(left, right):
    return lax.dot_general(
        left, right, (((0,), (0,)), ((), ())), preferred_element_type=jnp.float32
    )


def contract_last(left, right):
    return lax.dot_general(
        left, right, (((1,), (1,)), ((), ())), preferred_element_type=jnp.float32
    )


def gated_grads(gate_sum, up_sum, grad_hidden):
    sigmoid_gate = jax.nn.sigmoid(gate_sum)
    hidden = (gate_sum * sigmoid_gate * up_sum).astype(jnp.bfloat16)
    grad_up = (grad_hidden * gate_sum * sigmoid_gate).astype(jnp.bfloat16)
    grad_gate = (
        grad_hidden * up_sum * sigmoid_gate * (1.0 + gate_sum * (1.0 - sigmoid_gate))
    ).astype(jnp.bfloat16)
    return (hidden, grad_gate, grad_up)


def halving_reduce(x, order, n_dev):
    r = lax.axis_index("row")
    cur = x
    for step, bit in enumerate(order):
        n = cur.shape[1] // 2
        hi = (r // bit) % 2
        keep = lax.dynamic_slice_in_dim(cur, hi * n, n, 1)
        send = lax.dynamic_slice_in_dim(cur, (1 - hi) * n, n, 1)
        got = lax.ppermute(send, "row", [(j, j ^ bit) for j in range(n_dev)])
        cur = keep.astype(jnp.float32) + got.astype(jnp.float32)
        if step + 1 < len(order):
            cur = cur.astype(jnp.bfloat16)
    return cur


def doubling_gather(x, order, n_dev):
    r = lax.axis_index("row")
    cur = x
    for bit in reversed(order):
        hi = (r // bit) % 2
        got = lax.ppermute(cur, "row", [(j, j ^ bit) for j in range(n_dev)])
        cur = jnp.where(hi == 1, jnp.concatenate([got, cur], axis=1), jnp.concatenate([cur, got], axis=1))
    return cur


def row_bits(n_dev, tokens, units):
    if n_dev < 2 or n_dev & (n_dev - 1) or tokens % n_dev or units % 2:
        return None
    bits, b = [], 1
    while b < n_dev:
        bits.append(b)
        b *= 2
    return bits


def row_gated(stacked, n_dev):
    _, tokens, units = stacked.shape
    bits = row_bits(n_dev, tokens, units)
    if bits is None:
        sums = lax.psum(stacked, "row").astype(jnp.float32)
        return jnp.stack(gated_grads(sums[0], sums[1], sums[2]))
    orders = (bits, bits[:1] + bits[:0:-1])
    half = units // 2
    reduced = [halving_reduce(stacked[:, :, h * half:(h + 1) * half], o, n_dev) for h, o in enumerate(orders)]
    outs = [doubling_gather(jnp.stack(gated_grads(red[0], red[1], red[2])), o, n_dev) for red, o in zip(reduced, orders)]
    return jnp.concatenate(outs, axis=2)


def col_gather(x, n_col):
    parts = [x]
    for s in range(1, n_col):
        parts.append(lax.ppermute(x, "col", [(j, (j + s) % n_col) for j in range(n_col)]))
    return jnp.concatenate(parts, axis=0)


def col_reduce_scatter(x, n_col):
    span = x.shape[0] // n_col
    total = x[:span].astype(jnp.float32)
    for s in range(1, n_col):
        got = lax.ppermute(x[s * span:(s + 1) * span], "col", [(j, (j - s) % n_col) for j in range(n_col)])
        total = total + got.astype(jnp.float32)
    return total.astype(jnp.bfloat16)


def body(tokens, grad_out, gate_weight, up_weight, down_weight):
    n_row = lax.psum(1, "row")
    n_col = lax.psum(1, "col")
    tok_all = col_gather(tokens, n_col)
    grad_out, tok_all = lax.optimization_barrier((grad_out, tok_all))
    grad_all = col_gather(grad_out, n_col)
    tok_t = tok_all.T
    stacked = jnp.stack(
        [
            jnp.dot(tok_all, gate_weight, preferred_element_type=jnp.float32).astype(jnp.bfloat16),
            jnp.dot(tok_all, up_weight, preferred_element_type=jnp.float32).astype(jnp.bfloat16),
            contract_last(grad_all, down_weight).astype(jnp.bfloat16),
        ]
    )
    gated = row_gated(stacked, n_row)
    hidden, grad_gate, grad_up = gated[0], gated[1], gated[2]
    partial_grad = contract_last(grad_gate, gate_weight) + contract_last(grad_up, up_weight)
    partial_grad, grad_gate, grad_up, hidden = lax.optimization_barrier(
        (partial_grad.astype(jnp.bfloat16), grad_gate, grad_up, hidden)
    )
    acc_gate = jnp.dot(tok_t, grad_gate, preferred_element_type=jnp.float32).astype(jnp.bfloat16)
    partial_grad, acc_gate, grad_up, hidden = lax.optimization_barrier((partial_grad, acc_gate, grad_up, hidden))
    grad_tokens = col_reduce_scatter(partial_grad, n_col)
    acc_up = jnp.dot(tok_t, grad_up, preferred_element_type=jnp.float32)
    acc_down = contract_first(hidden, grad_all)
    return (
        grad_tokens,
        acc_gate,
        acc_up.astype(jnp.bfloat16),
        acc_down.astype(jnp.bfloat16),
    )


def solution(mesh):
    return jax.shard_map(
        body,
        mesh=mesh,
        in_specs=(
            P("col", "row"),
            P("col", "row"),
            P("row", "col"),
            P("row", "col"),
            P("col", "row"),
        ),
        out_specs=(P("col", "row"), P("row", "col"), P("row", "col"), P("col", "row")),
        check_vma=False,
    )
```

```python
import jax
import jax.numpy as jnp
from jax import lax
from jax.sharding import PartitionSpec as P


def contract_first(left, right):
    return lax.dot_general(
        left, right, (((0,), (0,)), ((), ())), preferred_element_type=jnp.float32
    )


def contract_last(left, right):
    return lax.dot_general(
        left, right, (((1,), (1,)), ((), ())), preferred_element_type=jnp.float32
    )


def gated_grads(gate_sum, up_sum, grad_hidden):
    sigmoid_gate = jax.nn.sigmoid(gate_sum)
    hidden = (gate_sum * sigmoid_gate * up_sum).astype(jnp.bfloat16)
    grad_up = (grad_hidden * gate_sum * sigmoid_gate).astype(jnp.bfloat16)
    grad_gate = (
        grad_hidden * up_sum * sigmoid_gate * (1.0 + gate_sum * (1.0 - sigmoid_gate))
    ).astype(jnp.bfloat16)
    return (hidden, grad_gate, grad_up)


def halving_reduce(parts, order, n_dev):
    r = lax.axis_index("row")
    cur = parts
    for step, bit in enumerate(order):
        axis = 0 if step == 0 else 1
        size = cur[0].shape[0] if step == 0 else cur.shape[1]
        n = size // 2
        hi = (r // bit) % 2
        perm = [(j, j ^ bit) for j in range(n_dev)]
        if step == 0:
            got = [lax.ppermute(lax.dynamic_slice_in_dim(c, (1 - hi) * n, n, 0), "row", perm) for c in cur]
            keep = [lax.dynamic_slice_in_dim(c, hi * n, n, 0) for c in cur]
            summed = jnp.stack([k.astype(jnp.float32) + g.astype(jnp.float32) for k, g in zip(keep, got)])
        else:
            keep = lax.dynamic_slice_in_dim(cur, hi * n, n, axis)
            send = lax.dynamic_slice_in_dim(cur, (1 - hi) * n, n, axis)
            got = lax.ppermute(send, "row", perm)
            summed = keep.astype(jnp.float32) + got.astype(jnp.float32)
        if step + 1 < len(order):
            summed = summed.astype(jnp.bfloat16)
        cur = summed
    return cur


def doubling_gather(x, order, n_dev):
    r = lax.axis_index("row")
    cur = x
    for bit in reversed(order):
        hi = (r // bit) % 2
        got = lax.ppermute(cur, "row", [(j, j ^ bit) for j in range(n_dev)])
        cur = jnp.where(hi == 1, jnp.concatenate([got, cur], axis=1), jnp.concatenate([cur, got], axis=1))
    return cur


def row_bits(n_dev, tokens, units):
    if n_dev < 2 or n_dev & (n_dev - 1) or tokens % n_dev or units % 2:
        return None
    bits, b = [], 1
    while b < n_dev:
        bits.append(b)
        b *= 2
    return bits


def row_gated(stacked, n_dev):
    tokens, units = stacked[0].shape
    bits = row_bits(n_dev, tokens, units)
    if bits is None:
        sums = lax.psum(jnp.stack(stacked), "row").astype(jnp.float32)
        return jnp.stack(gated_grads(sums[0], sums[1], sums[2]))
    orders = (bits, bits[:1] + bits[:0:-1])
    half = units // 2
    reduced = [halving_reduce([a[:, h * half:(h + 1) * half] for a in stacked], o, n_dev) for h, o in enumerate(orders)]
    outs = [doubling_gather(jnp.stack(gated_grads(red[0], red[1], red[2])), o, n_dev) for red, o in zip(reduced, orders)]
    return jnp.concatenate(outs, axis=2)


def col_gather(x, n_col):
    parts = [x]
    for s in range(1, n_col):
        parts.append(lax.ppermute(x, "col", [(j, (j + s) % n_col) for j in range(n_col)]))
    return jnp.concatenate(parts, axis=0)


def col_reduce_scatter(x, n_col):
    span = x.shape[0] // n_col
    total = x[:span].astype(jnp.float32)
    for s in range(1, n_col):
        got = lax.ppermute(x[s * span:(s + 1) * span], "col", [(j, (j - s) % n_col) for j in range(n_col)])
        total = total + got.astype(jnp.float32)
    return total.astype(jnp.bfloat16)


def body(tokens, grad_out, gate_weight, up_weight, down_weight):
    n_row = lax.psum(1, "row")
    n_col = lax.psum(1, "col")
    tok_all = col_gather(tokens, n_col)
    grad_out, tok_all = lax.optimization_barrier((grad_out, tok_all))
    grad_all = col_gather(grad_out, n_col)
    tok_t = tok_all.T
    stacked = [
        jnp.dot(tok_all, gate_weight, preferred_element_type=jnp.float32).astype(jnp.bfloat16),
        jnp.dot(tok_all, up_weight, preferred_element_type=jnp.float32).astype(jnp.bfloat16),
        contract_last(grad_all, down_weight).astype(jnp.bfloat16),
    ]
    gated = row_gated(stacked, n_row)
    hidden, grad_gate, grad_up = gated[0], gated[1], gated[2]
    partial_grad = contract_last(grad_gate, gate_weight) + contract_last(grad_up, up_weight)
    partial_grad, grad_gate, grad_up, hidden = lax.optimization_barrier(
        (partial_grad.astype(jnp.bfloat16), grad_gate, grad_up, hidden)
    )
    acc_gate = jnp.dot(tok_t, grad_gate, preferred_element_type=jnp.float32).astype(jnp.bfloat16)
    partial_grad, acc_gate, grad_up, hidden = lax.optimization_barrier((partial_grad, acc_gate, grad_up, hidden))
    grad_tokens = col_reduce_scatter(partial_grad, n_col)
    acc_up = jnp.dot(tok_t, grad_up, preferred_element_type=jnp.float32)
    acc_down = contract_first(hidden, grad_all)
    return (
        grad_tokens,
        acc_gate,
        acc_up.astype(jnp.bfloat16),
        acc_down.astype(jnp.bfloat16),
    )


def solution(mesh):
    return jax.shard_map(
        body,
        mesh=mesh,
        in_specs=(
            P("col", "row"),
            P("col", "row"),
            P("row", "col"),
            P("row", "col"),
            P("col", "row"),
        ),
        out_specs=(P("col", "row"), P("row", "col"), P("row", "col"), P("col", "row")),
        check_vma=False,
    )
```

```python
import jax
import jax.numpy as jnp
from jax import lax
from jax.sharding import PartitionSpec as P


def contract_first(left, right):
    return lax.dot_general(
        left, right, (((0,), (0,)), ((), ())), preferred_element_type=jnp.float32
    )


def contract_last(left, right):
    return lax.dot_general(
        left, right, (((1,), (1,)), ((), ())), preferred_element_type=jnp.float32
    )


def gated_grads(gate_sum, up_sum, grad_hidden):
    sigmoid_gate = jax.nn.sigmoid(gate_sum)
    hidden = (gate_sum * sigmoid_gate * up_sum).astype(jnp.bfloat16)
    grad_up = (grad_hidden * gate_sum * sigmoid_gate).astype(jnp.bfloat16)
    grad_gate = (
        grad_hidden * up_sum * sigmoid_gate * (1.0 + gate_sum * (1.0 - sigmoid_gate))
    ).astype(jnp.bfloat16)
    return (hidden, grad_gate, grad_up)


def halving_reduce(parts, order, n_dev):
    r = lax.axis_index("row")
    cur = parts
    for step, bit in enumerate(order):
        axis = 0 if step == 0 else 1
        size = cur[0].shape[0] if step == 0 else cur.shape[1]
        n = size // 2
        hi = (r // bit) % 2
        perm = [(j, j ^ bit) for j in range(n_dev)]
        if step == 0:
            got = [lax.ppermute(lax.dynamic_slice_in_dim(c, (1 - hi) * n, n, 0), "row", perm) for c in cur]
            keep = [lax.dynamic_slice_in_dim(c, hi * n, n, 0) for c in cur]
            summed = jnp.stack([k.astype(jnp.float32) + g.astype(jnp.float32) for k, g in zip(keep, got)])
        else:
            keep = lax.dynamic_slice_in_dim(cur, hi * n, n, axis)
            send = lax.dynamic_slice_in_dim(cur, (1 - hi) * n, n, axis)
            got = lax.ppermute(send, "row", perm)
            summed = keep.astype(jnp.float32) + got.astype(jnp.float32)
        if step + 1 < len(order):
            summed = summed.astype(jnp.bfloat16)
        cur = summed
    return cur


def doubling_gather(x, order, n_dev):
    r = lax.axis_index("row")
    cur = x
    for step, bit in enumerate(reversed(order)):
        hi = (r // bit) % 2
        perm = [(j, j ^ bit) for j in range(n_dev)]
        if step + 1 < len(order):
            got = lax.ppermute(cur, "row", perm)
            cur = jnp.where(hi == 1, jnp.concatenate([got, cur], axis=1), jnp.concatenate([cur, got], axis=1))
        else:
            out = []
            for i in (1, 2, 0):
                got = lax.ppermute(cur[i], "row", perm)
                out.append((i, jnp.where(hi == 1, jnp.concatenate([got, cur[i]], axis=0), jnp.concatenate([cur[i], got], axis=0))))
            cur = tuple(a for _, a in sorted(out))
    return cur


def row_bits(n_dev, tokens, units):
    if n_dev < 2 or n_dev & (n_dev - 1) or tokens % n_dev or units % 2:
        return None
    bits, b = [], 1
    while b < n_dev:
        bits.append(b)
        b *= 2
    return bits


def row_gated(stacked, n_dev):
    tokens, units = stacked[0].shape
    bits = row_bits(n_dev, tokens, units)
    if bits is None:
        sums = lax.psum(jnp.stack(stacked), "row").astype(jnp.float32)
        return gated_grads(sums[0], sums[1], sums[2])
    orders = (bits, bits[:1] + bits[:0:-1])
    half = units // 2
    reduced = [halving_reduce([a[:, h * half:(h + 1) * half] for a in stacked], o, n_dev) for h, o in enumerate(orders)]
    outs = [doubling_gather(jnp.stack(gated_grads(red[0], red[1], red[2])), o, n_dev) for red, o in zip(reduced, orders)]
    return tuple(jnp.concatenate([outs[0][i], outs[1][i]], axis=1) for i in range(3))


def col_gather(x, n_col):
    parts = [x]
    for s in range(1, n_col):
        parts.append(lax.ppermute(x, "col", [(j, (j + s) % n_col) for j in range(n_col)]))
    return jnp.concatenate(parts, axis=0)


def col_reduce_scatter(x, n_col):
    span = x.shape[0] // n_col
    total = x[:span].astype(jnp.float32)
    for s in range(1, n_col):
        got = lax.ppermute(x[s * span:(s + 1) * span], "col", [(j, (j - s) % n_col) for j in range(n_col)])
        total = total + got.astype(jnp.float32)
    return total.astype(jnp.bfloat16)


def body(tokens, grad_out, gate_weight, up_weight, down_weight):
    n_row = lax.psum(1, "row")
    n_col = lax.psum(1, "col")
    tok_all = col_gather(tokens, n_col)
    grad_out, tok_all = lax.optimization_barrier((grad_out, tok_all))
    grad_all = col_gather(grad_out, n_col)
    tok_t = tok_all.T
    stacked = [
        jnp.dot(tok_all, gate_weight, preferred_element_type=jnp.float32).astype(jnp.bfloat16),
        jnp.dot(tok_all, up_weight, preferred_element_type=jnp.float32).astype(jnp.bfloat16),
        contract_last(grad_all, down_weight).astype(jnp.bfloat16),
    ]
    gated = row_gated(stacked, n_row)
    hidden, grad_gate, grad_up = gated[0], gated[1], gated[2]
    partial_grad = contract_last(grad_gate, gate_weight) + contract_last(grad_up, up_weight)
    partial_grad, grad_gate, grad_up, hidden = lax.optimization_barrier(
        (partial_grad.astype(jnp.bfloat16), grad_gate, grad_up, hidden)
    )
    acc_gate = jnp.dot(tok_t, grad_gate, preferred_element_type=jnp.float32).astype(jnp.bfloat16)
    partial_grad, acc_gate, grad_up, hidden = lax.optimization_barrier((partial_grad, acc_gate, grad_up, hidden))
    grad_tokens = col_reduce_scatter(partial_grad, n_col)
    acc_up = jnp.dot(tok_t, grad_up, preferred_element_type=jnp.float32)
    acc_down = contract_first(hidden, grad_all)
    return (
        grad_tokens,
        acc_gate,
        acc_up.astype(jnp.bfloat16),
        acc_down.astype(jnp.bfloat16),
    )


def solution(mesh):
    return jax.shard_map(
        body,
        mesh=mesh,
        in_specs=(
            P("col", "row"),
            P("col", "row"),
            P("row", "col"),
            P("row", "col"),
            P("col", "row"),
        ),
        out_specs=(P("col", "row"), P("row", "col"), P("row", "col"), P("col", "row")),
        check_vma=False,
    )
```

```python
import jax
import jax.numpy as jnp
from jax import lax
from jax.sharding import PartitionSpec as P


def contract_first(left, right):
    return lax.dot_general(
        left, right, (((0,), (0,)), ((), ())), preferred_element_type=jnp.float32
    )


def contract_last(left, right):
    return lax.dot_general(
        left, right, (((1,), (1,)), ((), ())), preferred_element_type=jnp.float32
    )


def gated_grads(gate_sum, up_sum, grad_hidden):
    sigmoid_gate = jax.nn.sigmoid(gate_sum)
    hidden = (gate_sum * sigmoid_gate * up_sum).astype(jnp.bfloat16)
    grad_up = (grad_hidden * gate_sum * sigmoid_gate).astype(jnp.bfloat16)
    grad_gate = (
        grad_hidden * up_sum * sigmoid_gate * (1.0 + gate_sum * (1.0 - sigmoid_gate))
    ).astype(jnp.bfloat16)
    return (hidden, grad_gate, grad_up)


def halving_reduce(parts, order, n_dev):
    r = lax.axis_index("row")
    cur = parts
    for step, bit in enumerate(order):
        axis = 0 if step < PER_ARRAY_STEPS else 1
        size = cur[0].shape[0] if step < PER_ARRAY_STEPS else cur.shape[1]
        n = size // 2
        hi = (r // bit) % 2
        perm = [(j, j ^ bit) for j in range(n_dev)]
        if step < PER_ARRAY_STEPS:
            got = [lax.ppermute(lax.dynamic_slice_in_dim(c, (1 - hi) * n, n, 0), "row", perm) for c in cur]
            keep = [lax.dynamic_slice_in_dim(c, hi * n, n, 0) for c in cur]
            summed = [k.astype(jnp.float32) + g.astype(jnp.float32) for k, g in zip(keep, got)]
            if step + 1 == PER_ARRAY_STEPS or step + 1 == len(order):
                summed = jnp.stack(summed)
            elif step + 1 < len(order):
                summed = [a.astype(jnp.bfloat16) for a in summed]
                cur = summed
                continue
        else:
            keep = lax.dynamic_slice_in_dim(cur, hi * n, n, axis)
            send = lax.dynamic_slice_in_dim(cur, (1 - hi) * n, n, axis)
            got = lax.ppermute(send, "row", perm)
            summed = keep.astype(jnp.float32) + got.astype(jnp.float32)
        if step + 1 < len(order):
            summed = summed.astype(jnp.bfloat16)
        cur = summed
    return cur


PER_ARRAY_STEPS = 2


def doubling_gather(x, order, n_dev):
    r = lax.axis_index("row")
    cur = x
    for bit in reversed(order):
        hi = (r // bit) % 2
        got = lax.ppermute(cur, "row", [(j, j ^ bit) for j in range(n_dev)])
        cur = jnp.where(hi == 1, jnp.concatenate([got, cur], axis=1), jnp.concatenate([cur, got], axis=1))
    return cur


def row_bits(n_dev, tokens, units):
    if n_dev < 2 or n_dev & (n_dev - 1) or tokens % n_dev or units % 2:
        return None
    bits, b = [], 1
    while b < n_dev:
        bits.append(b)
        b *= 2
    return bits


def row_gated(stacked, n_dev):
    tokens, units = stacked[0].shape
    bits = row_bits(n_dev, tokens, units)
    if bits is None:
        sums = lax.psum(jnp.stack(stacked), "row").astype(jnp.float32)
        return jnp.stack(gated_grads(sums[0], sums[1], sums[2]))
    orders = (bits, bits[:1] + bits[:0:-1])
    half = units // 2
    reduced = [halving_reduce([a[:, h * half:(h + 1) * half] for a in stacked], o, n_dev) for h, o in enumerate(orders)]
    outs = [doubling_gather(jnp.stack(gated_grads(red[0], red[1], red[2])), o, n_dev) for red, o in zip(reduced, orders)]
    return jnp.concatenate(outs, axis=2)


def col_gather(x, n_col):
    parts = [x]
    for s in range(1, n_col):
        parts.append(lax.ppermute(x, "col", [(j, (j + s) % n_col) for j in range(n_col)]))
    return jnp.concatenate(parts, axis=0)


def col_reduce_scatter(x, n_col):
    span = x.shape[0] // n_col
    total = x[:span].astype(jnp.float32)
    for s in range(1, n_col):
        got = lax.ppermute(x[s * span:(s + 1) * span], "col", [(j, (j - s) % n_col) for j in range(n_col)])
        total = total + got.astype(jnp.float32)
    return total.astype(jnp.bfloat16)


def body(tokens, grad_out, gate_weight, up_weight, down_weight):
    n_row = lax.psum(1, "row")
    n_col = lax.psum(1, "col")
    tok_all = col_gather(tokens, n_col)
    grad_out, tok_all = lax.optimization_barrier((grad_out, tok_all))
    grad_all = col_gather(grad_out, n_col)
    tok_t = tok_all.T
    stacked = [
        jnp.dot(tok_all, gate_weight, preferred_element_type=jnp.float32).astype(jnp.bfloat16),
        jnp.dot(tok_all, up_weight, preferred_element_type=jnp.float32).astype(jnp.bfloat16),
        contract_last(grad_all, down_weight).astype(jnp.bfloat16),
    ]
    gated = row_gated(stacked, n_row)
    hidden, grad_gate, grad_up = gated[0], gated[1], gated[2]
    partial_grad = contract_last(grad_gate, gate_weight) + contract_last(grad_up, up_weight)
    partial_grad, grad_gate, grad_up, hidden = lax.optimization_barrier(
        (partial_grad.astype(jnp.bfloat16), grad_gate, grad_up, hidden)
    )
    acc_gate = jnp.dot(tok_t, grad_gate, preferred_element_type=jnp.float32).astype(jnp.bfloat16)
    partial_grad, acc_gate, grad_up, hidden = lax.optimization_barrier((partial_grad, acc_gate, grad_up, hidden))
    grad_tokens = col_reduce_scatter(partial_grad, n_col)
    acc_up = jnp.dot(tok_t, grad_up, preferred_element_type=jnp.float32)
    acc_down = contract_first(hidden, grad_all)
    return (
        grad_tokens,
        acc_gate,
        acc_up.astype(jnp.bfloat16),
        acc_down.astype(jnp.bfloat16),
    )


def solution(mesh):
    return jax.shard_map(
        body,
        mesh=mesh,
        in_specs=(
            P("col", "row"),
            P("col", "row"),
            P("row", "col"),
            P("row", "col"),
            P("col", "row"),
        ),
        out_specs=(P("col", "row"), P("row", "col"), P("row", "col"), P("col", "row")),
        check_vma=False,
    )
```

```python
import jax
import jax.numpy as jnp
from jax import lax
from jax.sharding import PartitionSpec as P


def contract_first(left, right):
    return lax.dot_general(
        left, right, (((0,), (0,)), ((), ())), preferred_element_type=jnp.float32
    )


def contract_last(left, right):
    return lax.dot_general(
        left, right, (((1,), (1,)), ((), ())), preferred_element_type=jnp.float32
    )


def gated_grads(gate_sum, up_sum, grad_hidden):
    sigmoid_gate = jax.nn.sigmoid(gate_sum)
    hidden = (gate_sum * sigmoid_gate * up_sum).astype(jnp.bfloat16)
    grad_up = (grad_hidden * gate_sum * sigmoid_gate).astype(jnp.bfloat16)
    grad_gate = (
        grad_hidden * up_sum * sigmoid_gate * (1.0 + gate_sum * (1.0 - sigmoid_gate))
    ).astype(jnp.bfloat16)
    return (hidden, grad_gate, grad_up)


def halving_reduce(parts, order, n_dev):
    r = lax.axis_index("row")
    cur = parts
    for step, bit in enumerate(order):
        axis = 0 if step < PER_ARRAY_STEPS else 1
        size = cur[0].shape[0] if step < PER_ARRAY_STEPS else cur.shape[1]
        n = size // 2
        hi = (r // bit) % 2
        perm = [(j, j ^ bit) for j in range(n_dev)]
        if step < PER_ARRAY_STEPS:
            got = [lax.ppermute(lax.dynamic_slice_in_dim(c, (1 - hi) * n, n, 0), "row", perm) for c in cur]
            keep = [lax.dynamic_slice_in_dim(c, hi * n, n, 0) for c in cur]
            summed = [k.astype(jnp.float32) + g.astype(jnp.float32) for k, g in zip(keep, got)]
            if step + 1 == PER_ARRAY_STEPS or step + 1 == len(order):
                summed = jnp.stack(summed)
            elif step + 1 < len(order):
                summed = [a.astype(jnp.bfloat16) for a in summed]
                cur = summed
                continue
        else:
            keep = lax.dynamic_slice_in_dim(cur, hi * n, n, axis)
            send = lax.dynamic_slice_in_dim(cur, (1 - hi) * n, n, axis)
            got = lax.ppermute(send, "row", perm)
            summed = keep.astype(jnp.float32) + got.astype(jnp.float32)
        if step + 1 < len(order):
            summed = summed.astype(jnp.bfloat16)
        cur = summed
    return cur


PER_ARRAY_STEPS = 3


def doubling_gather(x, order, n_dev):
    r = lax.axis_index("row")
    cur = x
    for bit in reversed(order):
        hi = (r // bit) % 2
        got = lax.ppermute(cur, "row", [(j, j ^ bit) for j in range(n_dev)])
        cur = jnp.where(hi == 1, jnp.concatenate([got, cur], axis=1), jnp.concatenate([cur, got], axis=1))
    return cur


def row_bits(n_dev, tokens, units):
    if n_dev < 2 or n_dev & (n_dev - 1) or tokens % n_dev or units % 2:
        return None
    bits, b = [], 1
    while b < n_dev:
        bits.append(b)
        b *= 2
    return bits


def row_gated(stacked, n_dev):
    tokens, units = stacked[0].shape
    bits = row_bits(n_dev, tokens, units)
    if bits is None:
        sums = lax.psum(jnp.stack(stacked), "row").astype(jnp.float32)
        return jnp.stack(gated_grads(sums[0], sums[1], sums[2]))
    orders = (bits, bits[:1] + bits[:0:-1])
    half = units // 2
    reduced = [halving_reduce([a[:, h * half:(h + 1) * half] for a in stacked], o, n_dev) for h, o in enumerate(orders)]
    outs = [doubling_gather(jnp.stack(gated_grads(red[0], red[1], red[2])), o, n_dev) for red, o in zip(reduced, orders)]
    return jnp.concatenate(outs, axis=2)


def col_gather(x, n_col):
    parts = [x]
    for s in range(1, n_col):
        parts.append(lax.ppermute(x, "col", [(j, (j + s) % n_col) for j in range(n_col)]))
    return jnp.concatenate(parts, axis=0)


def col_reduce_scatter(x, n_col):
    span = x.shape[0] // n_col
    total = x[:span].astype(jnp.float32)
    for s in range(1, n_col):
        got = lax.ppermute(x[s * span:(s + 1) * span], "col", [(j, (j - s) % n_col) for j in range(n_col)])
        total = total + got.astype(jnp.float32)
    return total.astype(jnp.bfloat16)


def body(tokens, grad_out, gate_weight, up_weight, down_weight):
    n_row = lax.psum(1, "row")
    n_col = lax.psum(1, "col")
    tok_all = col_gather(tokens, n_col)
    grad_out, tok_all = lax.optimization_barrier((grad_out, tok_all))
    grad_all = col_gather(grad_out, n_col)
    tok_t = tok_all.T
    stacked = [
        jnp.dot(tok_all, gate_weight, preferred_element_type=jnp.float32).astype(jnp.bfloat16),
        jnp.dot(tok_all, up_weight, preferred_element_type=jnp.float32).astype(jnp.bfloat16),
        contract_last(grad_all, down_weight).astype(jnp.bfloat16),
    ]
    gated = row_gated(stacked, n_row)
    hidden, grad_gate, grad_up = gated[0], gated[1], gated[2]
    partial_grad = contract_last(grad_gate, gate_weight) + contract_last(grad_up, up_weight)
    partial_grad, grad_gate, grad_up, hidden = lax.optimization_barrier(
        (partial_grad.astype(jnp.bfloat16), grad_gate, grad_up, hidden)
    )
    acc_gate = jnp.dot(tok_t, grad_gate, preferred_element_type=jnp.float32).astype(jnp.bfloat16)
    partial_grad, acc_gate, grad_up, hidden = lax.optimization_barrier((partial_grad, acc_gate, grad_up, hidden))
    grad_tokens = col_reduce_scatter(partial_grad, n_col)
    acc_up = jnp.dot(tok_t, grad_up, preferred_element_type=jnp.float32)
    acc_down = contract_first(hidden, grad_all)
    return (
        grad_tokens,
        acc_gate,
        acc_up.astype(jnp.bfloat16),
        acc_down.astype(jnp.bfloat16),
    )


def solution(mesh):
    return jax.shard_map(
        body,
        mesh=mesh,
        in_specs=(
            P("col", "row"),
            P("col", "row"),
            P("row", "col"),
            P("row", "col"),
            P("col", "row"),
        ),
        out_specs=(P("col", "row"), P("row", "col"), P("row", "col"), P("col", "row")),
        check_vma=False,
    )
```

```python
import jax
import jax.numpy as jnp
from jax import lax
from jax.sharding import PartitionSpec as P


def contract_first(left, right):
    return lax.dot_general(
        left, right, (((0,), (0,)), ((), ())), preferred_element_type=jnp.float32
    )


def contract_last(left, right):
    return lax.dot_general(
        left, right, (((1,), (1,)), ((), ())), preferred_element_type=jnp.float32
    )


def gated_grads(gate_sum, up_sum, grad_hidden):
    sigmoid_gate = jax.nn.sigmoid(gate_sum)
    hidden = (gate_sum * sigmoid_gate * up_sum).astype(jnp.bfloat16)
    grad_up = (grad_hidden * gate_sum * sigmoid_gate).astype(jnp.bfloat16)
    grad_gate = (
        grad_hidden * up_sum * sigmoid_gate * (1.0 + gate_sum * (1.0 - sigmoid_gate))
    ).astype(jnp.bfloat16)
    return (hidden, grad_gate, grad_up)


def halving_reduce(parts, order, n_dev):
    r = lax.axis_index("row")
    cur = parts
    for step, bit in enumerate(order):
        axis = 0 if step < PER_ARRAY_STEPS else 1
        size = cur[0].shape[0] if step < PER_ARRAY_STEPS else cur.shape[1]
        n = size // 2
        hi = (r // bit) % 2
        perm = [(j, j ^ bit) for j in range(n_dev)]
        if step < PER_ARRAY_STEPS:
            got = [lax.ppermute(lax.dynamic_slice_in_dim(c, (1 - hi) * n, n, 0), "row", perm) for c in cur]
            keep = [lax.dynamic_slice_in_dim(c, hi * n, n, 0) for c in cur]
            summed = [k.astype(jnp.float32) + g.astype(jnp.float32) for k, g in zip(keep, got)]
            if step + 1 == PER_ARRAY_STEPS or step + 1 == len(order):
                summed = jnp.stack(summed)
            elif step + 1 < len(order):
                summed = [a.astype(jnp.bfloat16) for a in summed]
                cur = summed
                continue
        else:
            keep = lax.dynamic_slice_in_dim(cur, hi * n, n, axis)
            send = lax.dynamic_slice_in_dim(cur, (1 - hi) * n, n, axis)
            got = lax.ppermute(send, "row", perm)
            summed = keep.astype(jnp.float32) + got.astype(jnp.float32)
        if step + 1 < len(order):
            summed = summed.astype(jnp.bfloat16)
        cur = summed
    return cur


PER_ARRAY_STEPS = 3


def doubling_gather(x, order, n_dev):
    r = lax.axis_index("row")
    cur = x
    for bit in reversed(order):
        hi = (r // bit) % 2
        got = lax.ppermute(cur, "row", [(j, j ^ bit) for j in range(n_dev)])
        cur = jnp.where(hi == 1, jnp.concatenate([got, cur], axis=1), jnp.concatenate([cur, got], axis=1))
    return cur


def row_bits(n_dev, tokens, units):
    if n_dev < 2 or n_dev & (n_dev - 1) or tokens % n_dev or units % 2:
        return None
    bits, b = [], 1
    while b < n_dev:
        bits.append(b)
        b *= 2
    return bits


def row_gated(stacked, n_dev):
    tokens, units = stacked[0].shape
    bits = row_bits(n_dev, tokens, units)
    if bits is None:
        sums = lax.psum(jnp.stack(stacked), "row").astype(jnp.float32)
        return jnp.stack(gated_grads(sums[0], sums[1], sums[2]))
    orders = (bits, bits[:1] + bits[:0:-1])
    half = units // 2
    reduced = [halving_reduce([a[:, h * half:(h + 1) * half] for a in stacked], o, n_dev) for h, o in enumerate(orders)]
    outs = [doubling_gather(jnp.stack(gated_grads(red[0], red[1], red[2])), o, n_dev) for red, o in zip(reduced, orders)]
    return jnp.concatenate(outs, axis=2)


def col_gather(x, n_col):
    parts = [x]
    for s in range(1, n_col):
        parts.append(lax.ppermute(x, "col", [(j, (j + s) % n_col) for j in range(n_col)]))
    return jnp.concatenate(parts, axis=0)


def col_reduce_scatter(x, n_col):
    span = x.shape[0] // n_col
    total = x[:span].astype(jnp.float32)
    for s in range(1, n_col):
        block = x[s * span:(s + 1) * span]
        left = lax.ppermute(block, "col", [(j, j - s) for j in range(s, n_col)])
        right = lax.ppermute(block, "col", [(j, j - s + n_col) for j in range(s)])
        total = total + left.astype(jnp.float32) + right.astype(jnp.float32)
    return total.astype(jnp.bfloat16)


def body(tokens, grad_out, gate_weight, up_weight, down_weight):
    n_row = lax.psum(1, "row")
    n_col = lax.psum(1, "col")
    tok_all = col_gather(tokens, n_col)
    grad_out, tok_all = lax.optimization_barrier((grad_out, tok_all))
    grad_all = col_gather(grad_out, n_col)
    tok_t = tok_all.T
    stacked = [
        jnp.dot(tok_all, gate_weight, preferred_element_type=jnp.float32).astype(jnp.bfloat16),
        jnp.dot(tok_all, up_weight, preferred_element_type=jnp.float32).astype(jnp.bfloat16),
        contract_last(grad_all, down_weight).astype(jnp.bfloat16),
    ]
    gated = row_gated(stacked, n_row)
    hidden, grad_gate, grad_up = gated[0], gated[1], gated[2]
    partial_grad = contract_last(grad_gate, gate_weight) + contract_last(grad_up, up_weight)
    partial_grad, grad_gate, grad_up, hidden = lax.optimization_barrier(
        (partial_grad.astype(jnp.bfloat16), grad_gate, grad_up, hidden)
    )
    acc_gate = jnp.dot(tok_t, grad_gate, preferred_element_type=jnp.float32).astype(jnp.bfloat16)
    partial_grad, acc_gate, grad_up, hidden = lax.optimization_barrier((partial_grad, acc_gate, grad_up, hidden))
    grad_tokens = col_reduce_scatter(partial_grad, n_col)
    acc_up = jnp.dot(tok_t, grad_up, preferred_element_type=jnp.float32)
    acc_down = contract_first(hidden, grad_all)
    return (
        grad_tokens,
        acc_gate,
        acc_up.astype(jnp.bfloat16),
        acc_down.astype(jnp.bfloat16),
    )


def solution(mesh):
    return jax.shard_map(
        body,
        mesh=mesh,
        in_specs=(
            P("col", "row"),
            P("col", "row"),
            P("row", "col"),
            P("row", "col"),
            P("col", "row"),
        ),
        out_specs=(P("col", "row"), P("row", "col"), P("row", "col"), P("col", "row")),
        check_vma=False,
    )
```

```python
import jax
import jax.numpy as jnp
from jax import lax
from jax.sharding import PartitionSpec as P


def contract_first(left, right):
    return lax.dot_general(
        left, right, (((0,), (0,)), ((), ())), preferred_element_type=jnp.float32
    )


def contract_last(left, right):
    return lax.dot_general(
        left, right, (((1,), (1,)), ((), ())), preferred_element_type=jnp.float32
    )


def gated_grads(gate_sum, up_sum, grad_hidden):
    sigmoid_gate = jax.nn.sigmoid(gate_sum)
    hidden = (gate_sum * sigmoid_gate * up_sum).astype(jnp.bfloat16)
    grad_up = (grad_hidden * gate_sum * sigmoid_gate).astype(jnp.bfloat16)
    grad_gate = (
        grad_hidden * up_sum * sigmoid_gate * (1.0 + gate_sum * (1.0 - sigmoid_gate))
    ).astype(jnp.bfloat16)
    return (hidden, grad_gate, grad_up)


def halving_reduce(parts, order, n_dev):
    r = lax.axis_index("row")
    cur = parts
    for step, bit in enumerate(order):
        axis = 0 if step < PER_ARRAY_STEPS else 1
        size = cur[0].shape[0] if step < PER_ARRAY_STEPS else cur.shape[1]
        n = size // 2
        hi = (r // bit) % 2
        perm = [(j, j ^ bit) for j in range(n_dev)]
        if step < PER_ARRAY_STEPS:
            got = [lax.ppermute(lax.dynamic_slice_in_dim(c, (1 - hi) * n, n, 0), "row", perm) for c in cur]
            keep = [lax.dynamic_slice_in_dim(c, hi * n, n, 0) for c in cur]
            summed = [k.astype(jnp.float32) + g.astype(jnp.float32) for k, g in zip(keep, got)]
            if step + 1 == PER_ARRAY_STEPS or step + 1 == len(order):
                summed = jnp.stack(summed)
            elif step + 1 < len(order):
                summed = [a.astype(jnp.bfloat16) for a in summed]
                cur = summed
                continue
        else:
            keep = lax.dynamic_slice_in_dim(cur, hi * n, n, axis)
            send = lax.dynamic_slice_in_dim(cur, (1 - hi) * n, n, axis)
            got = lax.ppermute(send, "row", perm)
            summed = keep.astype(jnp.float32) + got.astype(jnp.float32)
        if step + 1 < len(order):
            summed = summed.astype(jnp.bfloat16)
        cur = summed
    return cur


PER_ARRAY_STEPS = 3


def doubling_gather(x, order, n_dev):
    r = lax.axis_index("row")
    cur = x
    for bit in reversed(order):
        hi = (r // bit) % 2
        got = lax.ppermute(cur, "row", [(j, j ^ bit) for j in range(n_dev)])
        cur = jnp.where(hi == 1, jnp.concatenate([got, cur], axis=1), jnp.concatenate([cur, got], axis=1))
    return cur


def row_bits(n_dev, tokens, units):
    if n_dev < 2 or n_dev & (n_dev - 1) or tokens % n_dev or units % 2:
        return None
    bits, b = [], 1
    while b < n_dev:
        bits.append(b)
        b *= 2
    return bits


def row_gated(stacked, n_dev):
    tokens, units = stacked[0].shape
    bits = row_bits(n_dev, tokens, units)
    if bits is None:
        sums = lax.psum(jnp.stack(stacked), "row").astype(jnp.float32)
        return jnp.stack(gated_grads(sums[0], sums[1], sums[2]))
    orders = (bits, bits[:1] + bits[:0:-1])
    half = units // 2
    reduced = [halving_reduce([a[:, h * half:(h + 1) * half] for a in stacked], o, n_dev) for h, o in enumerate(orders)]
    outs = [doubling_gather(jnp.stack(gated_grads(red[0], red[1], red[2])), o, n_dev) for red, o in zip(reduced, orders)]
    return jnp.concatenate(outs, axis=2)


def col_gather(x, n_col):
    parts = [x]
    for s in range(1, n_col):
        parts.append(lax.ppermute(x, "col", [(j, (j + s) % n_col) for j in range(n_col)]))
    return jnp.concatenate(parts, axis=0)


def col_reduce_scatter(x, n_col):
    span = x.shape[0] // n_col
    total = x[:span].astype(jnp.float32)
    for s in range(1, n_col):
        got = lax.ppermute(x[s * span:(s + 1) * span], "col", [(j, (j - s) % n_col) for j in range(n_col)])
        total = total + got.astype(jnp.float32)
    return total.astype(jnp.bfloat16)


def body(tokens, grad_out, gate_weight, up_weight, down_weight):
    n_row = lax.psum(1, "row")
    n_col = lax.psum(1, "col")
    tok_all = col_gather(tokens, n_col)
    grad_all = col_gather(grad_out, n_col)
    tok_t = tok_all.T
    stacked = [
        jnp.dot(tok_all, gate_weight, preferred_element_type=jnp.float32).astype(jnp.bfloat16),
        jnp.dot(tok_all, up_weight, preferred_element_type=jnp.float32).astype(jnp.bfloat16),
        contract_last(grad_all, down_weight).astype(jnp.bfloat16),
    ]
    gated = row_gated(stacked, n_row)
    hidden, grad_gate, grad_up = gated[0], gated[1], gated[2]
    partial_grad = contract_last(grad_gate, gate_weight) + contract_last(grad_up, up_weight)
    partial_grad, grad_gate, grad_up, hidden = lax.optimization_barrier(
        (partial_grad.astype(jnp.bfloat16), grad_gate, grad_up, hidden)
    )
    acc_gate = jnp.dot(tok_t, grad_gate, preferred_element_type=jnp.float32).astype(jnp.bfloat16)
    partial_grad, acc_gate, grad_up, hidden = lax.optimization_barrier((partial_grad, acc_gate, grad_up, hidden))
    grad_tokens = col_reduce_scatter(partial_grad, n_col)
    acc_up = jnp.dot(tok_t, grad_up, preferred_element_type=jnp.float32)
    acc_down = contract_first(hidden, grad_all)
    return (
        grad_tokens,
        acc_gate,
        acc_up.astype(jnp.bfloat16),
        acc_down.astype(jnp.bfloat16),
    )


def solution(mesh):
    return jax.shard_map(
        body,
        mesh=mesh,
        in_specs=(
            P("col", "row"),
            P("col", "row"),
            P("row", "col"),
            P("row", "col"),
            P("col", "row"),
        ),
        out_specs=(P("col", "row"), P("row", "col"), P("row", "col"), P("col", "row")),
        check_vma=False,
    )
```

```python
import jax
import jax.numpy as jnp
from jax import lax
from jax.sharding import PartitionSpec as P


def contract_first(left, right):
    return lax.dot_general(
        left, right, (((0,), (0,)), ((), ())), preferred_element_type=jnp.float32
    )


def contract_last(left, right):
    return lax.dot_general(
        left, right, (((1,), (1,)), ((), ())), preferred_element_type=jnp.float32
    )


def gated_grads(gate_sum, up_sum, grad_hidden):
    sigmoid_gate = jax.nn.sigmoid(gate_sum)
    hidden = (gate_sum * sigmoid_gate * up_sum).astype(jnp.bfloat16)
    grad_up = (grad_hidden * gate_sum * sigmoid_gate).astype(jnp.bfloat16)
    grad_gate = (
        grad_hidden * up_sum * sigmoid_gate * (1.0 + gate_sum * (1.0 - sigmoid_gate))
    ).astype(jnp.bfloat16)
    return (hidden, grad_gate, grad_up)


def halving_reduce(parts, order, n_dev):
    r = lax.axis_index("row")
    cur = parts
    for step, bit in enumerate(order):
        axis = 0 if step < PER_ARRAY_STEPS else 1
        size = cur[0].shape[0] if step < PER_ARRAY_STEPS else cur.shape[1]
        n = size // 2
        hi = (r // bit) % 2
        perm = [(j, j ^ bit) for j in range(n_dev)]
        if step < PER_ARRAY_STEPS:
            got = [lax.ppermute(lax.dynamic_slice_in_dim(c, (1 - hi) * n, n, 0), "row", perm) for c in cur]
            keep = [lax.dynamic_slice_in_dim(c, hi * n, n, 0) for c in cur]
            summed = [k.astype(jnp.float32) + g.astype(jnp.float32) for k, g in zip(keep, got)]
            if step + 1 == PER_ARRAY_STEPS or step + 1 == len(order):
                summed = jnp.stack(summed)
            elif step + 1 < len(order):
                summed = [a.astype(jnp.bfloat16) for a in summed]
                cur = summed
                continue
        else:
            keep = lax.dynamic_slice_in_dim(cur, hi * n, n, axis)
            send = lax.dynamic_slice_in_dim(cur, (1 - hi) * n, n, axis)
            got = lax.ppermute(send, "row", perm)
            summed = keep.astype(jnp.float32) + got.astype(jnp.float32)
        if step + 1 < len(order):
            summed = summed.astype(jnp.bfloat16)
        cur = summed
    return cur


PER_ARRAY_STEPS = 3


def doubling_gather(x, order, n_dev):
    r = lax.axis_index("row")
    cur = list(x)
    for step, bit in enumerate(reversed(order)):
        hi = (r // bit) % 2
        perm = [(j, j ^ bit) for j in range(n_dev)]
        if step + 1 == len(order):
            cur = jnp.stack(cur)
            got = lax.ppermute(cur, "row", perm)
            cur = jnp.where(hi == 1, jnp.concatenate([got, cur], axis=1), jnp.concatenate([cur, got], axis=1))
        else:
            got = [lax.ppermute(c, "row", perm) for c in cur]
            cur = [jnp.where(hi == 1, jnp.concatenate([g, c], axis=0), jnp.concatenate([c, g], axis=0)) for c, g in zip(cur, got)]
    return cur


def row_bits(n_dev, tokens, units):
    if n_dev < 2 or n_dev & (n_dev - 1) or tokens % n_dev or units % 2:
        return None
    bits, b = [], 1
    while b < n_dev:
        bits.append(b)
        b *= 2
    return bits


def row_gated(stacked, n_dev):
    tokens, units = stacked[0].shape
    bits = row_bits(n_dev, tokens, units)
    if bits is None:
        sums = lax.psum(jnp.stack(stacked), "row").astype(jnp.float32)
        return jnp.stack(gated_grads(sums[0], sums[1], sums[2]))
    orders = (bits, bits[:1] + bits[:0:-1])
    half = units // 2
    reduced = [halving_reduce([a[:, h * half:(h + 1) * half] for a in stacked], o, n_dev) for h, o in enumerate(orders)]
    outs = [doubling_gather(gated_grads(red[0], red[1], red[2]), o, n_dev) for red, o in zip(reduced, orders)]
    return jnp.concatenate(outs, axis=2)


def col_gather(x, n_col):
    parts = [x]
    for s in range(1, n_col):
        parts.append(lax.ppermute(x, "col", [(j, (j + s) % n_col) for j in range(n_col)]))
    return jnp.concatenate(parts, axis=0)


def col_reduce_scatter(x, n_col):
    span = x.shape[0] // n_col
    total = x[:span].astype(jnp.float32)
    for s in range(1, n_col):
        got = lax.ppermute(x[s * span:(s + 1) * span], "col", [(j, (j - s) % n_col) for j in range(n_col)])
        total = total + got.astype(jnp.float32)
    return total.astype(jnp.bfloat16)


def body(tokens, grad_out, gate_weight, up_weight, down_weight):
    n_row = lax.psum(1, "row")
    n_col = lax.psum(1, "col")
    tok_all = col_gather(tokens, n_col)
    grad_out, tok_all = lax.optimization_barrier((grad_out, tok_all))
    grad_all = col_gather(grad_out, n_col)
    tok_t = tok_all.T
    stacked = [
        jnp.dot(tok_all, gate_weight, preferred_element_type=jnp.float32).astype(jnp.bfloat16),
        jnp.dot(tok_all, up_weight, preferred_element_type=jnp.float32).astype(jnp.bfloat16),
        contract_last(grad_all, down_weight).astype(jnp.bfloat16),
    ]
    gated = row_gated(stacked, n_row)
    hidden, grad_gate, grad_up = gated[0], gated[1], gated[2]
    partial_grad = contract_last(grad_gate, gate_weight) + contract_last(grad_up, up_weight)
    partial_grad, grad_gate, grad_up, hidden = lax.optimization_barrier(
        (partial_grad.astype(jnp.bfloat16), grad_gate, grad_up, hidden)
    )
    acc_gate = jnp.dot(tok_t, grad_gate, preferred_element_type=jnp.float32).astype(jnp.bfloat16)
    partial_grad, acc_gate, grad_up, hidden = lax.optimization_barrier((partial_grad, acc_gate, grad_up, hidden))
    grad_tokens = col_reduce_scatter(partial_grad, n_col)
    acc_up = jnp.dot(tok_t, grad_up, preferred_element_type=jnp.float32)
    acc_down = contract_first(hidden, grad_all)
    return (
        grad_tokens,
        acc_gate,
        acc_up.astype(jnp.bfloat16),
        acc_down.astype(jnp.bfloat16),
    )


def solution(mesh):
    return jax.shard_map(
        body,
        mesh=mesh,
        in_specs=(
            P("col", "row"),
            P("col", "row"),
            P("row", "col"),
            P("row", "col"),
            P("col", "row"),
        ),
        out_specs=(P("col", "row"), P("row", "col"), P("row", "col"), P("col", "row")),
        check_vma=False,
    )
```

```python
import jax
import jax.numpy as jnp
from jax import lax
from jax.sharding import PartitionSpec as P


def contract_first(left, right):
    return lax.dot_general(
        left, right, (((0,), (0,)), ((), ())), preferred_element_type=jnp.float32
    )


def contract_last(left, right):
    return lax.dot_general(
        left, right, (((1,), (1,)), ((), ())), preferred_element_type=jnp.float32
    )


def gated_grads(gate_sum, up_sum, grad_hidden):
    sigmoid_gate = jax.nn.sigmoid(gate_sum)
    hidden = (gate_sum * sigmoid_gate * up_sum).astype(jnp.bfloat16)
    grad_up = (grad_hidden * gate_sum * sigmoid_gate).astype(jnp.bfloat16)
    grad_gate = (
        grad_hidden * up_sum * sigmoid_gate * (1.0 + gate_sum * (1.0 - sigmoid_gate))
    ).astype(jnp.bfloat16)
    return (hidden, grad_gate, grad_up)


def halving_reduce(parts, order, n_dev):
    r = lax.axis_index("row")
    cur = parts
    for step, bit in enumerate(order):
        axis = 0 if step < PER_ARRAY_STEPS else 1
        size = cur[0].shape[0] if step < PER_ARRAY_STEPS else cur.shape[1]
        n = size // 2
        hi = (r // bit) % 2
        perm = [(j, j ^ bit) for j in range(n_dev)]
        if step < PER_ARRAY_STEPS:
            got = [lax.ppermute(lax.dynamic_slice_in_dim(c, (1 - hi) * n, n, 0), "row", perm) for c in cur]
            keep = [lax.dynamic_slice_in_dim(c, hi * n, n, 0) for c in cur]
            summed = [k.astype(jnp.float32) + g.astype(jnp.float32) for k, g in zip(keep, got)]
            if step + 1 == PER_ARRAY_STEPS or step + 1 == len(order):
                summed = jnp.stack(summed)
            elif step + 1 < len(order):
                summed = [a.astype(jnp.bfloat16) for a in summed]
                cur = summed
                continue
        else:
            keep = lax.dynamic_slice_in_dim(cur, hi * n, n, axis)
            send = lax.dynamic_slice_in_dim(cur, (1 - hi) * n, n, axis)
            got = lax.ppermute(send, "row", perm)
            summed = keep.astype(jnp.float32) + got.astype(jnp.float32)
        if step + 1 < len(order):
            summed = summed.astype(jnp.bfloat16)
        cur = summed
    return cur


PER_ARRAY_STEPS = 3


def doubling_gather(x, order, n_dev):
    r = lax.axis_index("row")
    cur = x
    for bit in reversed(order):
        hi = (r // bit) % 2
        got = lax.ppermute(cur, "row", [(j, j ^ bit) for j in range(n_dev)])
        cur = jnp.where(hi == 1, jnp.concatenate([got, cur], axis=1), jnp.concatenate([cur, got], axis=1))
    return cur


def row_bits(n_dev, tokens, units):
    if n_dev < 2 or n_dev & (n_dev - 1) or tokens % n_dev or units % 2:
        return None
    bits, b = [], 1
    while b < n_dev:
        bits.append(b)
        b *= 2
    return bits


def row_gated(stacked, n_dev):
    tokens, units = stacked[0].shape
    bits = row_bits(n_dev, tokens, units)
    if bits is None:
        sums = lax.psum(jnp.stack(stacked), "row").astype(jnp.float32)
        return jnp.stack(gated_grads(sums[0], sums[1], sums[2]))
    orders = (bits, bits[:1] + bits[:0:-1])
    half = units // 2
    reduced = [halving_reduce([a[:, h * half:(h + 1) * half] for a in stacked], o, n_dev) for h, o in enumerate(orders)]
    outs = [doubling_gather(jnp.stack(gated_grads(red[0], red[1], red[2])), o, n_dev) for red, o in zip(reduced, orders)]
    return jnp.concatenate(outs, axis=2)


def col_gather(x, n_col):
    parts = [x]
    for s in range(1, n_col):
        parts.append(lax.ppermute(x, "col", [(j, (j + s) % n_col) for j in range(n_col)]))
    return jnp.concatenate(parts, axis=0)


def col_reduce_scatter(x, n_col):
    span = x.shape[0] // n_col
    total = x[:span].astype(jnp.float32)
    for s in range(1, n_col):
        got = lax.ppermute(x[s * span:(s + 1) * span], "col", [(j, (j - s) % n_col) for j in range(n_col)])
        total = total + got.astype(jnp.float32)
    return total.astype(jnp.bfloat16)


def body(tokens, grad_out, gate_weight, up_weight, down_weight):
    n_row = lax.psum(1, "row")
    n_col = lax.psum(1, "col")
    tok_all = col_gather(tokens, n_col)
    grad_out, tok_all = lax.optimization_barrier((grad_out, tok_all))
    grad_all = col_gather(grad_out, n_col)
    tok_t = tok_all.T
    stacked = [
        jnp.dot(tok_all, gate_weight, preferred_element_type=jnp.float32).astype(jnp.bfloat16),
        jnp.dot(tok_all, up_weight, preferred_element_type=jnp.float32).astype(jnp.bfloat16),
        contract_last(grad_all, down_weight).astype(jnp.bfloat16),
    ]
    gated = row_gated(stacked, n_row)
    hidden, grad_gate, grad_up = gated[0], gated[1], gated[2]
    partial_grad = contract_last(grad_gate, gate_weight) + contract_last(grad_up, up_weight)
    partial_grad, grad_gate, grad_up, hidden = lax.optimization_barrier(
        (partial_grad.astype(jnp.bfloat16), grad_gate, grad_up, hidden)
    )
    grad_tokens = col_reduce_scatter(partial_grad, n_col)
    acc_gate = jnp.dot(tok_t, grad_gate, preferred_element_type=jnp.float32).astype(jnp.bfloat16)
    acc_up = jnp.dot(tok_t, grad_up, preferred_element_type=jnp.float32)
    acc_down = contract_first(hidden, grad_all)
    return (
        grad_tokens,
        acc_gate,
        acc_up.astype(jnp.bfloat16),
        acc_down.astype(jnp.bfloat16),
    )


def solution(mesh):
    return jax.shard_map(
        body,
        mesh=mesh,
        in_specs=(
            P("col", "row"),
            P("col", "row"),
            P("row", "col"),
            P("row", "col"),
            P("col", "row"),
        ),
        out_specs=(P("col", "row"), P("row", "col"), P("row", "col"), P("col", "row")),
        check_vma=False,
    )
```
